32 devices in a mesh: strip: 8 (over z, x), chan: 4 (over y, core).
Axes of the slice: x: 2, y: 2, z: 4, core: 2. Of those that a mesh axis runs over, the one named last changes fastest.
Arguments:
- features: bfloat16 [512, 32, 128], P('chan', 'strip'), may hold values from -6 to 6
- first_filters: bfloat16 [512, 3, 3, 512], P('chan'), may hold values from -0.09375 to 0.09375
- second_filters: bfloat16 [512, 3, 3, 512], P('chan'), may hold values from -0.09375 to 0.09375
- out_grad: bfloat16 [512, 32, 128], P('chan', 'strip'), may hold values from -6 to 6
Outputs:
- output: bfloat16 [512, 32, 128], P('chan', 'strip')
- input_grad: bfloat16 [512, 32, 128], P('chan', 'strip')
- first_grad: float32 [512, 3, 3, 512], P('chan')
- second_grad: float32 [512, 3, 3, 512], P('chan')
The draws below stay inside these ranges and needn't reach their ends.
All inputs are finite; a program needn't handle non-finite values.
Results may differ from the reference program's by a relative error of at most 0.005.
Values may be sent and summed in bfloat16 or wider, within the bound.
No kernel may reach another device: no remote copies, remote signals or barrier semaphores. Data moves between devices by JAX's collectives and lax.ppermute only.
A program may use at most 128 MiB of HBM per device.

```python
import jax
import jax.numpy as jnp
from jax import lax

C = 512
COLS = 128
ROWS = 32


def levels(stream_key, shape, cuts, low, high):
    level, own = 1.0, jax.random.fold_in(stream_key, 6)
    for dim, blocks in cuts:
        heights = jnp.exp(jax.random.uniform(jax.random.fold_in(own, dim), (blocks,), jnp.float32, low / len(cuts), high / len(cuts)))
        level = level * jnp.repeat(heights, shape[dim] // blocks).reshape([-1 if axis == dim else 1 for axis in range(len(shape))])
    return level


def normal_values(own_key, dims, width, bound, split=(), held_as=jnp.bfloat16):
    values = width * jax.random.normal(own_key, dims, jnp.float32)
    if split:
        values = values * levels(own_key, dims, split, -0.22, 0.18)
    return jnp.clip(values, -bound, bound).astype(held_as)


def setup_inputs(seed: int = 0) -> dict:
    splits = jax.random.split(jax.random.key(seed), 5)
    return {
        "features": normal_values(splits[0], (C, ROWS, COLS), 1.0, 6.0, ((0, 4), (1, 8))),
        "first_filters": normal_values(splits[1], (C, 3, 3, C), (9 * C) ** -0.5, 0.09375, ((0, 4),)),
        "second_filters": normal_values(splits[2], (C, 3, 3, C), (9 * C) ** -0.5, 0.09375, ((0, 4),)),
        "out_grad": normal_values(splits[3], (C, ROWS, COLS), 1.0, 6.0, ((0, 4), (1, 8))),
    }


def take_cols(field, shift):
    if shift == 0:
        return field
    edge = jnp.zeros(field.shape[:-1] + (1,), field.dtype)
    if shift > 0:
        return jnp.concatenate([field[..., 1:], edge], axis=-1)
    return jnp.concatenate([edge, field[..., :-1]], axis=-1)

def conv_fwd(padded, weight):
    chans, rows_pad, cols = padded.shape
    rows = rows_pad - 2
    outs = weight.shape[0]
    total = jnp.zeros((outs, rows, cols), jnp.float32)
    for kw in range(3):
        part = jnp.zeros((outs, rows * cols), jnp.float32)
        for kh in range(3):
            part = part + jnp.dot(weight[:, kh, kw, :], padded[:, kh:kh + rows, :].reshape(chans, rows * cols), preferred_element_type=jnp.float32)
        total = total + take_cols(part.reshape(outs, rows, cols), kw - 1)
    return total

def conv_back(padded, weight):
    outs, rows_pad, cols = padded.shape
    rows = rows_pad - 2
    inner = weight.shape[3]
    total = jnp.zeros((inner, rows, cols), jnp.float32)
    for kw in range(3):
        part = jnp.zeros((inner, rows * cols), jnp.float32)
        for kh in range(3):
            part = part + lax.dot_general(weight[:, kh, kw, :], padded[:, 2 - kh:2 - kh + rows, :].reshape(outs, rows * cols), (((0,), (0,)), ((), ())), preferred_element_type=jnp.float32)
        total = total + take_cols(part.reshape(inner, rows, cols), 1 - kw)
    return total

def filter_grad(grad_out, padded):
    outs, rows, cols = grad_out.shape
    chans = padded.shape[0]
    taps = []
    for kh in range(3):
        for kw in range(3):
            moved = take_cols(grad_out, 1 - kw).reshape(outs, rows * cols)
            taps.append(lax.dot_general(moved, padded[:, kh:kh + rows, :].reshape(chans, rows * cols), (((1,), (1,)), ((), ())), preferred_element_type=jnp.float32))
    return jnp.stack(taps, axis=1).reshape(outs, 3, 3, chans)

def pad_rows(field):
    return jnp.pad(field, ((0, 0), (1, 1), (0, 0)))

def reference(features, first_filters, second_filters, out_grad):
    x_pad = pad_rows(features)
    pre_full = conv_fwd(x_pad, first_filters)
    pre = pre_full.astype(jnp.bfloat16)
    hidden = jax.nn.silu(pre_full).astype(jnp.bfloat16)
    h_pad = pad_rows(hidden)
    output = (features.astype(jnp.float32) + conv_fwd(h_pad, second_filters)).astype(jnp.bfloat16)
    hidden_grad = conv_back(pad_rows(out_grad), second_filters)
    pre_val = pre.astype(jnp.float32)
    sig = jax.nn.sigmoid(pre_val)
    pre_grad = (hidden_grad * sig * (1.0 + pre_val * (1.0 - sig))).astype(jnp.bfloat16)
    input_grad = (out_grad.astype(jnp.float32) + conv_back(pad_rows(pre_grad), first_filters)).astype(jnp.bfloat16)
    second_grad = filter_grad(out_grad, h_pad)
    first_grad = filter_grad(pre_grad, x_pad)
    return (output, input_grad, first_grad, second_grad)
```

```python
import jax
import jax.numpy as jnp
from jax import lax
from jax.sharding import PartitionSpec as P


def extended(cells, sides, width):
    for axis, dim in sides:
        count = lax.axis_size(axis)
        ends = count - 1
        head = lax.slice_in_dim(cells, 0, width, axis=dim)
        tail = lax.slice_in_dim(cells, cells.shape[dim] - width, cells.shape[dim], axis=dim)
        cells = jnp.concatenate(
            [
                lax.ppermute(tail, axis, [(i, (i + 1) % count) for i in range(ends)]),
                cells,
                lax.ppermute(head, axis, [((i + 1) % count, i) for i in range(ends)]),
            ],
            axis=dim,
        )
    return cells


def take_cols(field, shift):
    if shift == 0:
        return field
    edge = jnp.zeros(field.shape[:-1] + (1,), field.dtype)
    if shift > 0:
        return jnp.concatenate([field[..., 1:], edge], axis=-1)
    return jnp.concatenate([edge, field[..., :-1]], axis=-1)


def conv_fwd(padded, weight):
    chans, rows_pad, cols = padded.shape
    rows = rows_pad - 2
    outs = weight.shape[0]
    flat_w = weight.reshape(outs * 9, chans)
    taps = jnp.dot(
        flat_w, padded.reshape(chans, rows_pad * cols), preferred_element_type=jnp.float32
    )
    taps = taps.reshape(outs, 3, 3, rows_pad, cols)
    total = jnp.zeros((outs, rows, cols), jnp.float32)
    for kh in range(3):
        for kw in range(3):
            total = total + take_cols(taps[:, kh, kw, kh : kh + rows, :], kw - 1)
    return total


def back_stack(padded):
    outs, rows_pad, cols = padded.shape
    rows = rows_pad - 2
    pieces = []
    for kh in range(3):
        for kw in range(3):
            pieces.append(take_cols(padded[:, 2 - kh : 2 - kh + rows, :], 1 - kw))
    return jnp.stack(pieces, axis=1).reshape(outs * 9, rows * cols)


def conv_back_stacked(stacked, weight, rows, cols):
    outs = weight.shape[0]
    inner = weight.shape[3]
    flat_w = weight.reshape(outs * 9, inner)
    result = lax.dot_general(
        flat_w, stacked, (((0,), (0,)), ((), ())), preferred_element_type=jnp.float32
    )
    return result.reshape(inner, rows, cols)


def filter_grad(grad_out, padded):
    outs, rows, cols = grad_out.shape
    chans, rows_pad, _ = padded.shape
    pieces = []
    for kh in range(3):
        for kw in range(3):
            moved = take_cols(grad_out, 1 - kw)
            pieces.append(jnp.pad(moved, ((0, 0), (kh, 2 - kh), (0, 0))))
    stacked = jnp.stack(pieces, axis=1).reshape(outs * 9, rows_pad * cols)
    result = lax.dot_general(
        stacked,
        padded.reshape(chans, rows_pad * cols),
        (((1,), (1,)), ((), ())),
        preferred_element_type=jnp.float32,
    )
    return result.reshape(outs, 3, 3, chans)


def chan_sum_scatter(part, axis):
    count = lax.axis_size(axis)
    me = lax.axis_index(axis)
    blocks = part.reshape((count, part.shape[0] // count) + part.shape[1:])
    bit = 1
    while bit < count:
        pairs = blocks.reshape((blocks.shape[0] // 2, 2) + blocks.shape[1:])
        side = (me // bit) % 2
        keep = lax.dynamic_index_in_dim(pairs, side, axis=1, keepdims=False)
        send = lax.dynamic_index_in_dim(pairs, 1 - side, axis=1, keepdims=False)
        blocks = keep + lax.ppermute(send, axis, [(i, i ^ bit) for i in range(count)])
        bit *= 2
    return blocks.reshape(blocks.shape[1:])


def body(features, first_filters, second_filters, out_grad):
    blocks, rows, cols = features.shape
    dy_pad = extended(out_grad, (("strip", 1),), 1)
    dy_stack = back_stack(dy_pad)
    hidden_grad = chan_sum_scatter(
        conv_back_stacked(dy_stack, second_filters, rows, cols), "chan"
    )
    x_pad = extended(features, (("strip", 1),), 1)
    x_all = lax.all_gather(x_pad, "chan", axis=0, tiled=True)
    pre_full = conv_fwd(x_all, first_filters)
    pre = pre_full.astype(jnp.bfloat16)
    hidden = jax.nn.silu(pre_full).astype(jnp.bfloat16)
    h_pad = extended(hidden, (("strip", 1),), 1)
    h_all = lax.all_gather(h_pad, "chan", axis=0, tiled=True)
    second_grad = lax.psum(filter_grad(out_grad, h_all), "strip")
    output = (features.astype(jnp.float32) + conv_fwd(h_all, second_filters)).astype(jnp.bfloat16)
    pre_val = pre.astype(jnp.float32)
    sig = jax.nn.sigmoid(pre_val)
    pre_grad = (hidden_grad * sig * (1.0 + pre_val * (1.0 - sig))).astype(jnp.bfloat16)
    da_pad = extended(pre_grad, (("strip", 1),), 1)
    second_grad, late_grad = lax.optimization_barrier((second_grad, pre_grad))
    first_grad = lax.psum(filter_grad(late_grad, x_all), "strip")
    da_stack = back_stack(da_pad)
    input_term = chan_sum_scatter(
        conv_back_stacked(da_stack, first_filters, rows, cols), "chan"
    )
    input_grad = (out_grad.astype(jnp.float32) + input_term).astype(jnp.bfloat16)
    return (output, input_grad, first_grad, second_grad)


def solution(mesh):
    in_specs = (
        P("chan", "strip", None),
        P("chan", None, None, None),
        P("chan", None, None, None),
        P("chan", "strip", None),
    )
    out_specs = (
        P("chan", "strip", None),
        P("chan", "strip", None),
        P("chan", None, None, None),
        P("chan", None, None, None),
    )
    return jax.shard_map(body, mesh=mesh, in_specs=in_specs, out_specs=out_specs, check_vma=False)
```

```python
import jax
import jax.numpy as jnp
from jax import lax
from jax.sharding import PartitionSpec as P


def extended(cells, sides, width):
    for axis, dim in sides:
        count = lax.axis_size(axis)
        ends = count - 1
        head = lax.slice_in_dim(cells, 0, width, axis=dim)
        tail = lax.slice_in_dim(cells, cells.shape[dim] - width, cells.shape[dim], axis=dim)
        cells = jnp.concatenate(
            [
                lax.ppermute(tail, axis, [(i, (i + 1) % count) for i in range(ends)]),
                cells,
                lax.ppermute(head, axis, [((i + 1) % count, i) for i in range(ends)]),
            ],
            axis=dim,
        )
    return cells


def take_cols(field, shift):
    if shift == 0:
        return field
    edge = jnp.zeros(field.shape[:-1] + (1,), field.dtype)
    if shift > 0:
        return jnp.concatenate([field[..., 1:], edge], axis=-1)
    return jnp.concatenate([edge, field[..., :-1]], axis=-1)


def conv_fwd(padded, weight):
    chans, rows_pad, cols = padded.shape
    rows = rows_pad - 2
    outs = weight.shape[0]
    flat_w = weight.reshape(outs * 9, chans)
    taps = jnp.dot(
        flat_w, padded.reshape(chans, rows_pad * cols), preferred_element_type=jnp.float32
    )
    taps = taps.reshape(outs, 3, 3, rows_pad, cols)
    total = jnp.zeros((outs, rows, cols), jnp.float32)
    for kh in range(3):
        for kw in range(3):
            total = total + take_cols(taps[:, kh, kw, kh : kh + rows, :], kw - 1)
    return total


def back_stack(padded):
    outs, rows_pad, cols = padded.shape
    rows = rows_pad - 2
    pieces = []
    for kh in range(3):
        for kw in range(3):
            pieces.append(take_cols(padded[:, 2 - kh : 2 - kh + rows, :], 1 - kw))
    return jnp.stack(pieces, axis=1).reshape(outs * 9, rows * cols)


def conv_back_stacked(stacked, weight, rows, cols):
    outs = weight.shape[0]
    inner = weight.shape[3]
    flat_w = weight.reshape(outs * 9, inner)
    result = lax.dot_general(
        flat_w, stacked, (((0,), (0,)), ((), ())), preferred_element_type=jnp.float32
    )
    return result.reshape(inner, rows, cols)


def filter_grad(grad_out, padded):
    outs, rows, cols = grad_out.shape
    chans, rows_pad, _ = padded.shape
    pieces = []
    for kh in range(3):
        for kw in range(3):
            moved = take_cols(grad_out, 1 - kw)
            pieces.append(jnp.pad(moved, ((0, 0), (kh, 2 - kh), (0, 0))))
    stacked = jnp.stack(pieces, axis=1).reshape(outs * 9, rows_pad * cols)
    result = lax.dot_general(
        stacked,
        padded.reshape(chans, rows_pad * cols),
        (((1,), (1,)), ((), ())),
        preferred_element_type=jnp.float32,
    )
    return result.reshape(outs, 3, 3, chans)


def chan_sum_scatter(part, axis):
    count = lax.axis_size(axis)
    me = lax.axis_index(axis)
    blocks = part.reshape((count, part.shape[0] // count) + part.shape[1:])
    bit = 1
    while bit < count:
        pairs = blocks.reshape((blocks.shape[0] // 2, 2) + blocks.shape[1:])
        side = (me // bit) % 2
        keep = lax.dynamic_index_in_dim(pairs, side, axis=1, keepdims=False)
        send = lax.dynamic_index_in_dim(pairs, 1 - side, axis=1, keepdims=False)
        blocks = keep + lax.ppermute(send, axis, [(i, i ^ bit) for i in range(count)])
        bit *= 2
    return blocks.reshape(blocks.shape[1:])


def halving_sum(flat, axis, bits):
    me = lax.axis_index(axis)
    count = lax.axis_size(axis)
    for bit in bits:
        pairs = flat.reshape(2, flat.shape[0] // 2)
        side = (me >> bit) & 1
        keep = lax.dynamic_index_in_dim(pairs, side, axis=0, keepdims=False)
        send = lax.dynamic_index_in_dim(pairs, 1 - side, axis=0, keepdims=False)
        flat = keep + lax.ppermute(send, axis, [(i, i ^ (1 << bit)) for i in range(count)])
    return flat


def halving_gather(part, axis, bits):
    me = lax.axis_index(axis)
    count = lax.axis_size(axis)
    for bit in reversed(bits):
        got = lax.ppermute(part, axis, [(i, i ^ (1 << bit)) for i in range(count)])
        side = (me >> bit) & 1
        part = jnp.where(side == 0, jnp.concatenate([part, got]), jnp.concatenate([got, part]))
    return part


def strip_allreduce(terms, axis):
    count = lax.axis_size(axis)
    levels = count.bit_length() - 1
    assert 1 << levels == count
    flat = jnp.concatenate([t.reshape(-1) for t in terms])
    half = flat.shape[0] // 2
    orders = (tuple(range(levels)), tuple(range(1, levels)) + (0,))
    outs = []
    for part, bits in zip((flat[:half], flat[half:]), orders):
        summed = halving_sum(part, axis, bits).astype(jnp.bfloat16)
        outs.append(halving_gather(summed, axis, bits))
    flat = jnp.concatenate(outs).astype(jnp.float32)
    results, at = [], 0
    for t in terms:
        results.append(flat[at : at + t.size].reshape(t.shape))
        at += t.size
    return results


def body(features, first_filters, second_filters, out_grad):
    blocks, rows, cols = features.shape
    dy_pad = extended(out_grad, (("strip", 1),), 1)
    dy_stack = back_stack(dy_pad)
    hidden_grad = chan_sum_scatter(
        conv_back_stacked(dy_stack, second_filters, rows, cols), "chan"
    )
    x_pad = extended(features, (("strip", 1),), 1)
    x_all = lax.all_gather(x_pad, "chan", axis=0, tiled=True)
    pre_full = conv_fwd(x_all, first_filters)
    pre = pre_full.astype(jnp.bfloat16)
    hidden = jax.nn.silu(pre_full).astype(jnp.bfloat16)
    h_pad = extended(hidden, (("strip", 1),), 1)
    h_all = lax.all_gather(h_pad, "chan", axis=0, tiled=True)
    second_part = filter_grad(out_grad, h_all)
    output = (features.astype(jnp.float32) + conv_fwd(h_all, second_filters)).astype(jnp.bfloat16)
    pre_val = pre.astype(jnp.float32)
    sig = jax.nn.sigmoid(pre_val)
    pre_grad = (hidden_grad * sig * (1.0 + pre_val * (1.0 - sig))).astype(jnp.bfloat16)
    da_pad = extended(pre_grad, (("strip", 1),), 1)
    first_grad, second_grad = strip_allreduce((filter_grad(pre_grad, x_all), second_part), "strip")
    da_stack = back_stack(da_pad)
    input_term = chan_sum_scatter(
        conv_back_stacked(da_stack, first_filters, rows, cols), "chan"
    )
    input_grad = (out_grad.astype(jnp.float32) + input_term).astype(jnp.bfloat16)
    return (output, input_grad, first_grad, second_grad)


def solution(mesh):
    in_specs = (
        P("chan", "strip", None),
        P("chan", None, None, None),
        P("chan", None, None, None),
        P("chan", "strip", None),
    )
    out_specs = (
        P("chan", "strip", None),
        P("chan", "strip", None),
        P("chan", None, None, None),
        P("chan", None, None, None),
    )
    return jax.shard_map(body, mesh=mesh, in_specs=in_specs, out_specs=out_specs, check_vma=False)
```

```python
import jax
import jax.numpy as jnp
from jax import lax
from jax.sharding import PartitionSpec as P


def extended(cells, sides, width):
    for axis, dim in sides:
        count = lax.axis_size(axis)
        ends = count - 1
        head = lax.slice_in_dim(cells, 0, width, axis=dim)
        tail = lax.slice_in_dim(cells, cells.shape[dim] - width, cells.shape[dim], axis=dim)
        cells = jnp.concatenate(
            [
                lax.ppermute(tail, axis, [(i, (i + 1) % count) for i in range(ends)]),
                cells,
                lax.ppermute(head, axis, [((i + 1) % count, i) for i in range(ends)]),
            ],
            axis=dim,
        )
    return cells


def take_cols(field, shift):
    if shift == 0:
        return field
    edge = jnp.zeros(field.shape[:-1] + (1,), field.dtype)
    if shift > 0:
        return jnp.concatenate([field[..., 1:], edge], axis=-1)
    return jnp.concatenate([edge, field[..., :-1]], axis=-1)


def conv_fwd(padded, weight):
    chans, rows_pad, cols = padded.shape
    rows = rows_pad - 2
    outs = weight.shape[0]
    flat_w = weight.reshape(outs * 9, chans)
    taps = jnp.dot(
        flat_w, padded.reshape(chans, rows_pad * cols), preferred_element_type=jnp.float32
    )
    taps = taps.reshape(outs, 3, 3, rows_pad, cols)
    total = jnp.zeros((outs, rows, cols), jnp.float32)
    for kh in range(3):
        for kw in range(3):
            total = total + take_cols(taps[:, kh, kw, kh : kh + rows, :], kw - 1)
    return total


def back_stack(padded):
    outs, rows_pad, cols = padded.shape
    rows = rows_pad - 2
    pieces = []
    for kh in range(3):
        for kw in range(3):
            pieces.append(take_cols(padded[:, 2 - kh : 2 - kh + rows, :], 1 - kw))
    return jnp.stack(pieces, axis=1).reshape(outs * 9, rows * cols)


def conv_back_stacked(stacked, weight, rows, cols):
    outs = weight.shape[0]
    inner = weight.shape[3]
    flat_w = weight.reshape(outs * 9, inner)
    result = lax.dot_general(
        flat_w, stacked, (((0,), (0,)), ((), ())), preferred_element_type=jnp.float32
    )
    return result.reshape(inner, rows, cols)


def filter_grad(grad_out, padded):
    outs, rows, cols = grad_out.shape
    chans, rows_pad, _ = padded.shape
    pieces = []
    for kh in range(3):
        for kw in range(3):
            moved = take_cols(grad_out, 1 - kw)
            pieces.append(jnp.pad(moved, ((0, 0), (kh, 2 - kh), (0, 0))))
    stacked = jnp.stack(pieces, axis=1).reshape(outs * 9, rows_pad * cols)
    result = lax.dot_general(
        stacked,
        padded.reshape(chans, rows_pad * cols),
        (((1,), (1,)), ((), ())),
        preferred_element_type=jnp.float32,
    )
    return result.reshape(outs, 3, 3, chans)


def chan_sum_scatter(part, axis):
    count = lax.axis_size(axis)
    me = lax.axis_index(axis)
    blocks = part.reshape((count, part.shape[0] // count) + part.shape[1:])
    bit = 1
    while bit < count:
        pairs = blocks.reshape((blocks.shape[0] // 2, 2) + blocks.shape[1:])
        side = (me // bit) % 2
        keep = lax.dynamic_index_in_dim(pairs, side, axis=1, keepdims=False)
        send = lax.dynamic_index_in_dim(pairs, 1 - side, axis=1, keepdims=False)
        blocks = keep + lax.ppermute(send, axis, [(i, i ^ bit) for i in range(count)])
        bit *= 2
    return blocks.reshape(blocks.shape[1:])


def halving_sum(flat, axis, bits):
    me = lax.axis_index(axis)
    count = lax.axis_size(axis)
    for bit in bits:
        pairs = flat.reshape(2, flat.shape[0] // 2)
        side = (me >> bit) & 1
        keep = lax.dynamic_index_in_dim(pairs, side, axis=0, keepdims=False)
        send = lax.dynamic_index_in_dim(pairs, 1 - side, axis=0, keepdims=False)
        flat = keep + lax.ppermute(send, axis, [(i, i ^ (1 << bit)) for i in range(count)])
    return flat


def halving_gather(part, axis, bits):
    me = lax.axis_index(axis)
    count = lax.axis_size(axis)
    for bit in reversed(bits):
        got = lax.ppermute(part, axis, [(i, i ^ (1 << bit)) for i in range(count)])
        side = (me >> bit) & 1
        part = jnp.where(side == 0, jnp.concatenate([part, got]), jnp.concatenate([got, part]))
    return part


def strip_allreduce(terms, axis):
    count = lax.axis_size(axis)
    levels = count.bit_length() - 1
    assert 1 << levels == count
    flat = jnp.concatenate([t.reshape(-1) for t in terms])
    half = flat.shape[0] // 2
    orders = (tuple(range(levels)), tuple(range(1, levels)) + (0,))
    outs = []
    for part, bits in zip((flat[:half], flat[half:]), orders):
        summed = halving_sum(part, axis, bits).astype(jnp.bfloat16)
        outs.append(halving_gather(summed, axis, bits))
    flat = jnp.concatenate(outs).astype(jnp.float32)
    results, at = [], 0
    for t in terms:
        results.append(flat[at : at + t.size].reshape(t.shape))
        at += t.size
    return results


def body(features, first_filters, second_filters, out_grad):
    blocks, rows, cols = features.shape
    dy_pad = extended(out_grad, (("strip", 1),), 1)
    dy_stack = back_stack(dy_pad)
    hidden_grad = chan_sum_scatter(
        conv_back_stacked(dy_stack, second_filters, rows, cols), "chan"
    )
    x_pad = extended(features, (("strip", 1),), 1)
    x_all = lax.all_gather(x_pad, "chan", axis=0, tiled=True)
    pre_full = conv_fwd(x_all, first_filters)
    pre = pre_full.astype(jnp.bfloat16)
    hidden = jax.nn.silu(pre_full).astype(jnp.bfloat16)
    h_pad = extended(hidden, (("strip", 1),), 1)
    h_all = lax.all_gather(h_pad, "chan", axis=0, tiled=True)
    (second_grad,) = strip_allreduce((filter_grad(out_grad, h_all),), "strip")
    output = (features.astype(jnp.float32) + conv_fwd(h_all, second_filters)).astype(jnp.bfloat16)
    pre_val = pre.astype(jnp.float32)
    sig = jax.nn.sigmoid(pre_val)
    pre_grad = (hidden_grad * sig * (1.0 + pre_val * (1.0 - sig))).astype(jnp.bfloat16)
    da_pad = extended(pre_grad, (("strip", 1),), 1)
    (first_grad,) = strip_allreduce((filter_grad(pre_grad, x_all),), "strip")
    da_stack = back_stack(da_pad)
    input_term = chan_sum_scatter(
        conv_back_stacked(da_stack, first_filters, rows, cols), "chan"
    )
    input_grad = (out_grad.astype(jnp.float32) + input_term).astype(jnp.bfloat16)
    return (output, input_grad, first_grad, second_grad)


def solution(mesh):
    in_specs = (
        P("chan", "strip", None),
        P("chan", None, None, None),
        P("chan", None, None, None),
        P("chan", "strip", None),
    )
    out_specs = (
        P("chan", "strip", None),
        P("chan", "strip", None),
        P("chan", None, None, None),
        P("chan", None, None, None),
    )
    return jax.shard_map(body, mesh=mesh, in_specs=in_specs, out_specs=out_specs, check_vma=False)
```

```python
import jax
import jax.numpy as jnp
from jax import lax
from jax.sharding import PartitionSpec as P


def extended(cells, sides, width):
    for axis, dim in sides:
        count = lax.axis_size(axis)
        ends = count - 1
        head = lax.slice_in_dim(cells, 0, width, axis=dim)
        tail = lax.slice_in_dim(cells, cells.shape[dim] - width, cells.shape[dim], axis=dim)
        cells = jnp.concatenate(
            [
                lax.ppermute(tail, axis, [(i, (i + 1) % count) for i in range(ends)]),
                cells,
                lax.ppermute(head, axis, [((i + 1) % count, i) for i in range(ends)]),
            ],
            axis=dim,
        )
    return cells


def take_cols(field, shift):
    if shift == 0:
        return field
    edge = jnp.zeros(field.shape[:-1] + (1,), field.dtype)
    if shift > 0:
        return jnp.concatenate([field[..., 1:], edge], axis=-1)
    return jnp.concatenate([edge, field[..., :-1]], axis=-1)


def im2col(padded):
    chans, rows_pad, cols = padded.shape
    rows = rows_pad - 2
    pieces = []
    for kh in range(3):
        for kw in range(3):
            pieces.append(take_cols(padded[:, kh : kh + rows, :], kw - 1))
    return jnp.stack(pieces, axis=0).reshape(9 * chans, rows * cols)


def conv_fwd(cols_in, weight, rows, cols):
    outs = weight.shape[0]
    flat_w = weight.reshape(outs, -1)
    total = jnp.dot(flat_w, cols_in, preferred_element_type=jnp.float32)
    return total.reshape(outs, rows, cols)


def back_stack(padded):
    outs, rows_pad, cols = padded.shape
    rows = rows_pad - 2
    pieces = []
    for kh in range(3):
        for kw in range(3):
            pieces.append(take_cols(padded[:, 2 - kh : 2 - kh + rows, :], 1 - kw))
    return jnp.stack(pieces, axis=1).reshape(outs * 9, rows * cols)


def conv_back_stacked(stacked, weight, rows, cols):
    outs = weight.shape[0]
    inner = weight.shape[3]
    flat_w = weight.reshape(outs * 9, inner)
    result = lax.dot_general(
        flat_w, stacked, (((0,), (0,)), ((), ())), preferred_element_type=jnp.float32
    )
    return result.reshape(inner, rows, cols)


def filter_grad(grad_out, cols_in):
    outs, rows, cols = grad_out.shape
    result = lax.dot_general(
        grad_out.reshape(outs, rows * cols),
        cols_in,
        (((1,), (1,)), ((), ())),
        preferred_element_type=jnp.float32,
    )
    return result.reshape(outs, 3, 3, cols_in.shape[0] // 9)


def chan_sum_scatter(part, axis):
    count = lax.axis_size(axis)
    me = lax.axis_index(axis)
    blocks = part.reshape((count, part.shape[0] // count) + part.shape[1:])
    bit = 1
    while bit < count:
        pairs = blocks.reshape((blocks.shape[0] // 2, 2) + blocks.shape[1:])
        side = (me // bit) % 2
        keep = lax.dynamic_index_in_dim(pairs, side, axis=1, keepdims=False)
        send = lax.dynamic_index_in_dim(pairs, 1 - side, axis=1, keepdims=False)
        blocks = keep + lax.ppermute(send, axis, [(i, i ^ bit) for i in range(count)])
        bit *= 2
    return blocks.reshape(blocks.shape[1:])


def halving_sum(flat, axis, bits):
    me = lax.axis_index(axis)
    count = lax.axis_size(axis)
    for bit in bits:
        pairs = flat.reshape(2, flat.shape[0] // 2)
        side = (me >> bit) & 1
        keep = lax.dynamic_index_in_dim(pairs, side, axis=0, keepdims=False)
        send = lax.dynamic_index_in_dim(pairs, 1 - side, axis=0, keepdims=False)
        flat = keep + lax.ppermute(send, axis, [(i, i ^ (1 << bit)) for i in range(count)])
    return flat


def halving_gather(part, axis, bits):
    me = lax.axis_index(axis)
    count = lax.axis_size(axis)
    for bit in reversed(bits):
        got = lax.ppermute(part, axis, [(i, i ^ (1 << bit)) for i in range(count)])
        side = (me >> bit) & 1
        part = jnp.where(side == 0, jnp.concatenate([part, got]), jnp.concatenate([got, part]))
    return part


def strip_allreduce(terms, axis):
    count = lax.axis_size(axis)
    levels = count.bit_length() - 1
    assert 1 << levels == count
    flat = jnp.concatenate([t.reshape(-1) for t in terms])
    half = flat.shape[0] // 2
    orders = (tuple(range(levels)), tuple(range(1, levels)) + (0,))
    outs = []
    for part, bits in zip((flat[:half], flat[half:]), orders):
        summed = halving_sum(part, axis, bits).astype(jnp.bfloat16)
        outs.append(halving_gather(summed, axis, bits))
    flat = jnp.concatenate(outs).astype(jnp.float32)
    results, at = [], 0
    for t in terms:
        results.append(flat[at : at + t.size].reshape(t.shape))
        at += t.size
    return results


def body(features, first_filters, second_filters, out_grad):
    blocks, rows, cols = features.shape
    dy_pad = extended(out_grad, (("strip", 1),), 1)
    dy_stack = back_stack(dy_pad)
    hidden_grad = chan_sum_scatter(
        conv_back_stacked(dy_stack, second_filters, rows, cols), "chan"
    )
    x_pad = extended(features, (("strip", 1),), 1)
    x_all = lax.all_gather(x_pad, "chan", axis=0, tiled=True)
    x_cols = im2col(x_all)
    pre_full = conv_fwd(x_cols, first_filters, rows, cols)
    pre = pre_full.astype(jnp.bfloat16)
    hidden = jax.nn.silu(pre_full).astype(jnp.bfloat16)
    h_pad = extended(hidden, (("strip", 1),), 1)
    h_all = lax.all_gather(h_pad, "chan", axis=0, tiled=True)
    h_cols = im2col(h_all)
    (second_grad,) = strip_allreduce((filter_grad(out_grad, h_cols),), "strip")
    output = (features.astype(jnp.float32) + conv_fwd(h_cols, second_filters, rows, cols)).astype(jnp.bfloat16)
    pre_val = pre.astype(jnp.float32)
    sig = jax.nn.sigmoid(pre_val)
    pre_grad = (hidden_grad * sig * (1.0 + pre_val * (1.0 - sig))).astype(jnp.bfloat16)
    da_pad = extended(pre_grad, (("strip", 1),), 1)
    (first_grad,) = strip_allreduce((filter_grad(pre_grad, x_cols),), "strip")
    da_stack = back_stack(da_pad)
    input_term = chan_sum_scatter(
        conv_back_stacked(da_stack, first_filters, rows, cols), "chan"
    )
    input_grad = (out_grad.astype(jnp.float32) + input_term).astype(jnp.bfloat16)
    return (output, input_grad, first_grad, second_grad)


def solution(mesh):
    in_specs = (
        P("chan", "strip", None),
        P("chan", None, None, None),
        P("chan", None, None, None),
        P("chan", "strip", None),
    )
    out_specs = (
        P("chan", "strip", None),
        P("chan", "strip", None),
        P("chan", None, None, None),
        P("chan", None, None, None),
    )
    return jax.shard_map(body, mesh=mesh, in_specs=in_specs, out_specs=out_specs, check_vma=False)
```

```python
import jax
import jax.numpy as jnp
from jax import lax
from jax.sharding import PartitionSpec as P


def extended(cells, sides, width):
    for axis, dim in sides:
        count = lax.axis_size(axis)
        ends = count - 1
        head = lax.slice_in_dim(cells, 0, width, axis=dim)
        tail = lax.slice_in_dim(cells, cells.shape[dim] - width, cells.shape[dim], axis=dim)
        cells = jnp.concatenate(
            [
                lax.ppermute(tail, axis, [(i, (i + 1) % count) for i in range(ends)]),
                cells,
                lax.ppermute(head, axis, [((i + 1) % count, i) for i in range(ends)]),
            ],
            axis=dim,
        )
    return cells


def take_cols(field, shift):
    if shift == 0:
        return field
    edge = jnp.zeros(field.shape[:-1] + (1,), field.dtype)
    if shift > 0:
        return jnp.concatenate([field[..., 1:], edge], axis=-1)
    return jnp.concatenate([edge, field[..., :-1]], axis=-1)


def im2col(padded):
    chans, rows_pad, cols = padded.shape
    rows = rows_pad - 2
    pieces = []
    for kh in range(3):
        for kw in range(3):
            pieces.append(take_cols(padded[:, kh : kh + rows, :], kw - 1))
    return jnp.stack(pieces, axis=0).reshape(9 * chans, rows * cols)


def conv_fwd(cols_in, weight, rows, cols):
    outs = weight.shape[0]
    flat_w = weight.reshape(outs, -1)
    total = jnp.dot(flat_w, cols_in, preferred_element_type=jnp.float32)
    return total.reshape(outs, rows, cols)


def back_stack(padded):
    outs, rows_pad, cols = padded.shape
    rows = rows_pad - 2
    pieces = []
    for kh in range(3):
        for kw in range(3):
            pieces.append(take_cols(padded[:, 2 - kh : 2 - kh + rows, :], 1 - kw))
    return jnp.stack(pieces, axis=1).reshape(outs * 9, rows * cols)


def conv_back_stacked(stacked, weight, rows, cols):
    outs = weight.shape[0]
    inner = weight.shape[3]
    flat_w = weight.reshape(outs * 9, inner)
    result = lax.dot_general(
        flat_w, stacked, (((0,), (0,)), ((), ())), preferred_element_type=jnp.float32
    )
    return result.reshape(inner, rows, cols)


def filter_grad(grad_out, cols_in):
    outs, rows, cols = grad_out.shape
    result = lax.dot_general(
        grad_out.reshape(outs, rows * cols),
        cols_in,
        (((1,), (1,)), ((), ())),
        preferred_element_type=jnp.float32,
    )
    return result.reshape(outs, 3, 3, cols_in.shape[0] // 9)


def chan_sum_scatter(part, axis):
    count = lax.axis_size(axis)
    me = lax.axis_index(axis)
    blocks = part.reshape((count, part.shape[0] // count) + part.shape[1:])
    bit = 1
    while bit < count:
        pairs = blocks.reshape((blocks.shape[0] // 2, 2) + blocks.shape[1:])
        side = (me // bit) % 2
        keep = lax.dynamic_index_in_dim(pairs, side, axis=1, keepdims=False)
        send = lax.dynamic_index_in_dim(pairs, 1 - side, axis=1, keepdims=False)
        blocks = keep + lax.ppermute(send, axis, [(i, i ^ bit) for i in range(count)])
        bit *= 2
    return blocks.reshape(blocks.shape[1:])


def halving_sum(flat, axis, bits):
    me = lax.axis_index(axis)
    count = lax.axis_size(axis)
    for bit in bits:
        pairs = flat.reshape(2, flat.shape[0] // 2)
        side = (me >> bit) & 1
        keep = lax.dynamic_index_in_dim(pairs, side, axis=0, keepdims=False)
        send = lax.dynamic_index_in_dim(pairs, 1 - side, axis=0, keepdims=False)
        flat = keep + lax.ppermute(send, axis, [(i, i ^ (1 << bit)) for i in range(count)])
    return flat


def halving_gather(part, axis, bits):
    me = lax.axis_index(axis)
    count = lax.axis_size(axis)
    for bit in reversed(bits):
        got = lax.ppermute(part, axis, [(i, i ^ (1 << bit)) for i in range(count)])
        side = (me >> bit) & 1
        part = jnp.where(side == 0, jnp.concatenate([part, got]), jnp.concatenate([got, part]))
    return part


def chan_gather(block, axis):
    levels = lax.axis_size(axis).bit_length() - 1
    return halving_gather(block, axis, tuple(reversed(range(levels))))


def strip_allreduce(terms, axis):
    count = lax.axis_size(axis)
    levels = count.bit_length() - 1
    assert 1 << levels == count
    flat = jnp.concatenate([t.reshape(-1) for t in terms])
    half = flat.shape[0] // 2
    orders = (tuple(range(levels)), tuple(range(1, levels)) + (0,))
    outs = []
    for part, bits in zip((flat[:half], flat[half:]), orders):
        summed = halving_sum(part, axis, bits).astype(jnp.bfloat16)
        outs.append(halving_gather(summed, axis, bits))
    flat = jnp.concatenate(outs).astype(jnp.float32)
    results, at = [], 0
    for t in terms:
        results.append(flat[at : at + t.size].reshape(t.shape))
        at += t.size
    return results


def body(features, first_filters, second_filters, out_grad):
    blocks, rows, cols = features.shape
    dy_pad = extended(out_grad, (("strip", 1),), 1)
    dy_stack = back_stack(dy_pad)
    hidden_grad = chan_sum_scatter(
        conv_back_stacked(dy_stack, second_filters, rows, cols), "chan"
    )
    x_pad = extended(features, (("strip", 1),), 1)
    x_all = chan_gather(x_pad, "chan")
    x_cols = im2col(x_all)
    pre_full = conv_fwd(x_cols, first_filters, rows, cols)
    pre = pre_full.astype(jnp.bfloat16)
    hidden = jax.nn.silu(pre_full).astype(jnp.bfloat16)
    h_pad = extended(hidden, (("strip", 1),), 1)
    h_all = chan_gather(h_pad, "chan")
    h_cols = im2col(h_all)
    (second_grad,) = strip_allreduce((filter_grad(out_grad, h_cols),), "strip")
    output = (features.astype(jnp.float32) + conv_fwd(h_cols, second_filters, rows, cols)).astype(jnp.bfloat16)
    pre_val = pre.astype(jnp.float32)
    sig = jax.nn.sigmoid(pre_val)
    pre_grad = (hidden_grad * sig * (1.0 + pre_val * (1.0 - sig))).astype(jnp.bfloat16)
    da_pad = extended(pre_grad, (("strip", 1),), 1)
    (first_grad,) = strip_allreduce((filter_grad(pre_grad, x_cols),), "strip")
    da_stack = back_stack(da_pad)
    input_term = chan_sum_scatter(
        conv_back_stacked(da_stack, first_filters, rows, cols), "chan"
    )
    input_grad = (out_grad.astype(jnp.float32) + input_term).astype(jnp.bfloat16)
    return (output, input_grad, first_grad, second_grad)


def solution(mesh):
    in_specs = (
        P("chan", "strip", None),
        P("chan", None, None, None),
        P("chan", None, None, None),
        P("chan", "strip", None),
    )
    out_specs = (
        P("chan", "strip", None),
        P("chan", "strip", None),
        P("chan", None, None, None),
        P("chan", None, None, None),
    )
    return jax.shard_map(body, mesh=mesh, in_specs=in_specs, out_specs=out_specs, check_vma=False)
```

```python
import jax
import jax.numpy as jnp
from jax import lax
from jax.sharding import PartitionSpec as P


def extended(cells, sides, width):
    for axis, dim in sides:
        count = lax.axis_size(axis)
        ends = count - 1
        head = lax.slice_in_dim(cells, 0, width, axis=dim)
        tail = lax.slice_in_dim(cells, cells.shape[dim] - width, cells.shape[dim], axis=dim)
        cells = jnp.concatenate(
            [
                lax.ppermute(tail, axis, [(i, (i + 1) % count) for i in range(ends)]),
                cells,
                lax.ppermute(head, axis, [((i + 1) % count, i) for i in range(ends)]),
            ],
            axis=dim,
        )
    return cells


def take_cols(field, shift):
    if shift == 0:
        return field
    edge = jnp.zeros(field.shape[:-1] + (1,), field.dtype)
    if shift > 0:
        return jnp.concatenate([field[..., 1:], edge], axis=-1)
    return jnp.concatenate([edge, field[..., :-1]], axis=-1)


def im2col(padded):
    chans, rows_pad, cols = padded.shape
    rows = rows_pad - 2
    pieces = []
    for kh in range(3):
        for kw in range(3):
            pieces.append(take_cols(padded[:, kh : kh + rows, :], kw - 1))
    return jnp.stack(pieces, axis=0).reshape(9 * chans, rows * cols)


def conv_fwd(cols_in, weight, rows, cols):
    outs = weight.shape[0]
    flat_w = weight.reshape(outs, -1)
    total = jnp.dot(flat_w, cols_in, preferred_element_type=jnp.float32)
    return total.reshape(outs, rows, cols)


def back_stack(padded):
    outs, rows_pad, cols = padded.shape
    rows = rows_pad - 2
    pieces = []
    for kh in range(3):
        for kw in range(3):
            pieces.append(take_cols(padded[:, 2 - kh : 2 - kh + rows, :], 1 - kw))
    return jnp.stack(pieces, axis=1).reshape(outs * 9, rows * cols)


def conv_back_stacked(stacked, weight, rows, cols):
    outs = weight.shape[0]
    inner = weight.shape[3]
    flat_w = weight.reshape(outs * 9, inner)
    result = lax.dot_general(
        flat_w, stacked, (((0,), (0,)), ((), ())), preferred_element_type=jnp.float32
    )
    return result.reshape(inner, rows, cols)


def filter_grad(grad_out, cols_in):
    outs, rows, cols = grad_out.shape
    result = lax.dot_general(
        grad_out.reshape(outs, rows * cols),
        cols_in,
        (((1,), (1,)), ((), ())),
        preferred_element_type=jnp.float32,
    )
    return result.reshape(outs, 3, 3, cols_in.shape[0] // 9)


def chan_sum_scatter(part, axis):
    count = lax.axis_size(axis)
    me = lax.axis_index(axis)
    blocks = part.reshape((count, part.shape[0] // count) + part.shape[1:])
    bit = 1
    while bit < count:
        pairs = blocks.reshape((blocks.shape[0] // 2, 2) + blocks.shape[1:])
        side = (me // bit) % 2
        keep = lax.dynamic_index_in_dim(pairs, side, axis=1, keepdims=False)
        send = lax.dynamic_index_in_dim(pairs, 1 - side, axis=1, keepdims=False)
        blocks = keep + lax.ppermute(send, axis, [(i, i ^ bit) for i in range(count)])
        bit *= 2
    return blocks.reshape(blocks.shape[1:])


def halving_sum(flat, axis, bits):
    me = lax.axis_index(axis)
    count = lax.axis_size(axis)
    for bit in bits:
        pairs = flat.reshape(2, flat.shape[0] // 2)
        side = (me >> bit) & 1
        keep = lax.dynamic_index_in_dim(pairs, side, axis=0, keepdims=False)
        send = lax.dynamic_index_in_dim(pairs, 1 - side, axis=0, keepdims=False)
        flat = keep + lax.ppermute(send, axis, [(i, i ^ (1 << bit)) for i in range(count)])
    return flat


def halving_gather(part, axis, bits):
    me = lax.axis_index(axis)
    count = lax.axis_size(axis)
    for bit in reversed(bits):
        got = lax.ppermute(part, axis, [(i, i ^ (1 << bit)) for i in range(count)])
        side = (me >> bit) & 1
        part = jnp.where(side == 0, jnp.concatenate([part, got]), jnp.concatenate([got, part]))
    return part


def chan_gather(block, axis):
    levels = lax.axis_size(axis).bit_length() - 1
    return halving_gather(block, axis, tuple(reversed(range(levels))))


def strip_allreduce(terms, axis):
    count = lax.axis_size(axis)
    levels = count.bit_length() - 1
    assert 1 << levels == count
    flat = jnp.concatenate([t.reshape(-1) for t in terms])
    tracks = min(levels, 3)
    size = flat.shape[0] // tracks
    assert size * tracks == flat.shape[0] and size % count == 0
    base = tuple(range(levels))
    outs = []
    for k in range(tracks):
        bits = base[k:] + base[:k]
        summed = halving_sum(flat[k * size : (k + 1) * size], axis, bits).astype(jnp.bfloat16)
        outs.append(halving_gather(summed, axis, bits))
    flat = jnp.concatenate(outs).astype(jnp.float32)
    results, at = [], 0
    for t in terms:
        results.append(flat[at : at + t.size].reshape(t.shape))
        at += t.size
    return results


def body(features, first_filters, second_filters, out_grad):
    blocks, rows, cols = features.shape
    dy_pad = extended(out_grad, (("strip", 1),), 1)
    dy_stack = back_stack(dy_pad)
    hidden_grad = chan_sum_scatter(
        conv_back_stacked(dy_stack, second_filters, rows, cols), "chan"
    )
    x_pad = extended(features, (("strip", 1),), 1)
    x_all = chan_gather(x_pad, "chan")
    x_cols = im2col(x_all)
    pre_full = conv_fwd(x_cols, first_filters, rows, cols)
    pre = pre_full.astype(jnp.bfloat16)
    hidden = jax.nn.silu(pre_full).astype(jnp.bfloat16)
    h_pad = extended(hidden, (("strip", 1),), 1)
    h_all = chan_gather(h_pad, "chan")
    h_cols = im2col(h_all)
    (second_grad,) = strip_allreduce((filter_grad(out_grad, h_cols),), "strip")
    output = (features.astype(jnp.float32) + conv_fwd(h_cols, second_filters, rows, cols)).astype(jnp.bfloat16)
    pre_val = pre.astype(jnp.float32)
    sig = jax.nn.sigmoid(pre_val)
    pre_grad = (hidden_grad * sig * (1.0 + pre_val * (1.0 - sig))).astype(jnp.bfloat16)
    da_pad = extended(pre_grad, (("strip", 1),), 1)
    (first_grad,) = strip_allreduce((filter_grad(pre_grad, x_cols),), "strip")
    da_stack = back_stack(da_pad)
    input_term = chan_sum_scatter(
        conv_back_stacked(da_stack, first_filters, rows, cols), "chan"
    )
    input_grad = (out_grad.astype(jnp.float32) + input_term).astype(jnp.bfloat16)
    return (output, input_grad, first_grad, second_grad)


def solution(mesh):
    in_specs = (
        P("chan", "strip", None),
        P("chan", None, None, None),
        P("chan", None, None, None),
        P("chan", "strip", None),
    )
    out_specs = (
        P("chan", "strip", None),
        P("chan", "strip", None),
        P("chan", None, None, None),
        P("chan", None, None, None),
    )
    return jax.shard_map(body, mesh=mesh, in_specs=in_specs, out_specs=out_specs, check_vma=False)
```

```python
import jax
import jax.numpy as jnp
from jax import lax
from jax.sharding import PartitionSpec as P


def extended(cells, sides, width):
    for axis, dim in sides:
        count = lax.axis_size(axis)
        ends = count - 1
        head = lax.slice_in_dim(cells, 0, width, axis=dim)
        tail = lax.slice_in_dim(cells, cells.shape[dim] - width, cells.shape[dim], axis=dim)
        cells = jnp.concatenate(
            [
                lax.ppermute(tail, axis, [(i, (i + 1) % count) for i in range(ends)]),
                cells,
                lax.ppermute(head, axis, [((i + 1) % count, i) for i in range(ends)]),
            ],
            axis=dim,
        )
    return cells


def take_cols(field, shift):
    if shift == 0:
        return field
    edge = jnp.zeros(field.shape[:-1] + (1,), field.dtype)
    if shift > 0:
        return jnp.concatenate([field[..., 1:], edge], axis=-1)
    return jnp.concatenate([edge, field[..., :-1]], axis=-1)


def im2col(padded):
    chans, rows_pad, cols = padded.shape
    rows = rows_pad - 2
    pieces = []
    for kh in range(3):
        for kw in range(3):
            pieces.append(take_cols(padded[:, kh : kh + rows, :], kw - 1))
    return jnp.stack(pieces, axis=0).reshape(9 * chans, rows * cols)


def conv_fwd(cols_in, weight, rows, cols):
    outs = weight.shape[0]
    flat_w = weight.reshape(outs, -1)
    total = jnp.dot(flat_w, cols_in, preferred_element_type=jnp.float32)
    return total.reshape(outs, rows, cols)


def back_stack(padded):
    outs, rows_pad, cols = padded.shape
    rows = rows_pad - 2
    pieces = []
    for kh in range(3):
        for kw in range(3):
            pieces.append(take_cols(padded[:, 2 - kh : 2 - kh + rows, :], 1 - kw))
    return jnp.stack(pieces, axis=1).reshape(outs * 9, rows * cols)


def conv_back_stacked(stacked, weight, rows, cols):
    outs = weight.shape[0]
    inner = weight.shape[3]
    flat_w = weight.reshape(outs * 9, inner)
    result = lax.dot_general(
        flat_w, stacked, (((0,), (0,)), ((), ())), preferred_element_type=jnp.float32
    )
    return result.reshape(inner, rows, cols)


def filter_grad(grad_out, cols_in):
    outs, rows, cols = grad_out.shape
    result = lax.dot_general(
        grad_out.reshape(outs, rows * cols),
        cols_in,
        (((1,), (1,)), ((), ())),
        preferred_element_type=jnp.float32,
    )
    return result.reshape(outs, 3, 3, cols_in.shape[0] // 9)


def chan_sum_scatter(part, axis):
    count = lax.axis_size(axis)
    me = lax.axis_index(axis)
    blocks = part.reshape((count, part.shape[0] // count) + part.shape[1:])
    bit = 1
    while bit < count:
        pairs = blocks.reshape((blocks.shape[0] // 2, 2) + blocks.shape[1:])
        side = (me // bit) % 2
        keep = lax.dynamic_index_in_dim(pairs, side, axis=1, keepdims=False)
        send = lax.dynamic_index_in_dim(pairs, 1 - side, axis=1, keepdims=False)
        blocks = keep + lax.ppermute(send, axis, [(i, i ^ bit) for i in range(count)])
        bit *= 2
    return blocks.reshape(blocks.shape[1:])


def halving_sum(flat, axis, bits):
    me = lax.axis_index(axis)
    count = lax.axis_size(axis)
    for bit in bits:
        pairs = flat.reshape(2, flat.shape[0] // 2)
        side = (me >> bit) & 1
        keep = lax.dynamic_index_in_dim(pairs, side, axis=0, keepdims=False)
        send = lax.dynamic_index_in_dim(pairs, 1 - side, axis=0, keepdims=False)
        flat = keep + lax.ppermute(send, axis, [(i, i ^ (1 << bit)) for i in range(count)])
    return flat


def halving_gather(part, axis, bits):
    me = lax.axis_index(axis)
    count = lax.axis_size(axis)
    for bit in reversed(bits):
        got = lax.ppermute(part, axis, [(i, i ^ (1 << bit)) for i in range(count)])
        side = (me >> bit) & 1
        part = jnp.where(side == 0, jnp.concatenate([part, got]), jnp.concatenate([got, part]))
    return part


def chan_gather(block, axis):
    levels = lax.axis_size(axis).bit_length() - 1
    return halving_gather(block, axis, tuple(reversed(range(levels))))


def strip_allreduce(terms, axis):
    count = lax.axis_size(axis)
    levels = count.bit_length() - 1
    assert 1 << levels == count
    flat = jnp.concatenate([t.reshape(-1) for t in terms])
    half = flat.shape[0] // 2
    orders = (tuple(range(levels)), (1, 0) + tuple(range(2, levels)))
    outs = []
    for part, bits in zip((flat[:half], flat[half:]), orders):
        summed = halving_sum(part, axis, bits).astype(jnp.bfloat16)
        outs.append(halving_gather(summed, axis, bits))
    flat = jnp.concatenate(outs).astype(jnp.float32)
    results, at = [], 0
    for t in terms:
        results.append(flat[at : at + t.size].reshape(t.shape))
        at += t.size
    return results


def body(features, first_filters, second_filters, out_grad):
    blocks, rows, cols = features.shape
    dy_pad = extended(out_grad, (("strip", 1),), 1)
    dy_stack = back_stack(dy_pad)
    hidden_grad = chan_sum_scatter(
        conv_back_stacked(dy_stack, second_filters, rows, cols), "chan"
    )
    x_pad = extended(features, (("strip", 1),), 1)
    x_all = chan_gather(x_pad, "chan")
    x_cols = im2col(x_all)
    pre_full = conv_fwd(x_cols, first_filters, rows, cols)
    pre = pre_full.astype(jnp.bfloat16)
    hidden = jax.nn.silu(pre_full).astype(jnp.bfloat16)
    h_pad = extended(hidden, (("strip", 1),), 1)
    h_all = chan_gather(h_pad, "chan")
    h_cols = im2col(h_all)
    (second_grad,) = strip_allreduce((filter_grad(out_grad, h_cols),), "strip")
    output = (features.astype(jnp.float32) + conv_fwd(h_cols, second_filters, rows, cols)).astype(jnp.bfloat16)
    pre_val = pre.astype(jnp.float32)
    sig = jax.nn.sigmoid(pre_val)
    pre_grad = (hidden_grad * sig * (1.0 + pre_val * (1.0 - sig))).astype(jnp.bfloat16)
    da_pad = extended(pre_grad, (("strip", 1),), 1)
    (first_grad,) = strip_allreduce((filter_grad(pre_grad, x_cols),), "strip")
    da_stack = back_stack(da_pad)
    input_term = chan_sum_scatter(
        conv_back_stacked(da_stack, first_filters, rows, cols), "chan"
    )
    input_grad = (out_grad.astype(jnp.float32) + input_term).astype(jnp.bfloat16)
    return (output, input_grad, first_grad, second_grad)


def solution(mesh):
    in_specs = (
        P("chan", "strip", None),
        P("chan", None, None, None),
        P("chan", None, None, None),
        P("chan", "strip", None),
    )
    out_specs = (
        P("chan", "strip", None),
        P("chan", "strip", None),
        P("chan", None, None, None),
        P("chan", None, None, None),
    )
    return jax.shard_map(body, mesh=mesh, in_specs=in_specs, out_specs=out_specs, check_vma=False)
```

```python
import jax
import jax.numpy as jnp
from jax import lax
from jax.sharding import PartitionSpec as P


def extended(cells, sides, width):
    for axis, dim in sides:
        count = lax.axis_size(axis)
        ends = count - 1
        head = lax.slice_in_dim(cells, 0, width, axis=dim)
        tail = lax.slice_in_dim(cells, cells.shape[dim] - width, cells.shape[dim], axis=dim)
        cells = jnp.concatenate(
            [
                lax.ppermute(tail, axis, [(i, (i + 1) % count) for i in range(ends)]),
                cells,
                lax.ppermute(head, axis, [((i + 1) % count, i) for i in range(ends)]),
            ],
            axis=dim,
        )
    return cells


def take_cols(field, shift):
    if shift == 0:
        return field
    edge = jnp.zeros(field.shape[:-1] + (1,), field.dtype)
    if shift > 0:
        return jnp.concatenate([field[..., 1:], edge], axis=-1)
    return jnp.concatenate([edge, field[..., :-1]], axis=-1)


def im2col(padded):
    chans, rows_pad, cols = padded.shape
    rows = rows_pad - 2
    pieces = []
    for kh in range(3):
        for kw in range(3):
            pieces.append(take_cols(padded[:, kh : kh + rows, :], kw - 1))
    return jnp.stack(pieces, axis=0).reshape(9 * chans, rows * cols)


def conv_fwd(cols_in, weight, rows, cols):
    outs = weight.shape[0]
    flat_w = weight.reshape(outs, -1)
    total = jnp.dot(flat_w, cols_in, preferred_element_type=jnp.float32)
    return total.reshape(outs, rows, cols)


def back_stack(padded):
    outs, rows_pad, cols = padded.shape
    rows = rows_pad - 2
    pieces = []
    for kh in range(3):
        for kw in range(3):
            pieces.append(take_cols(padded[:, 2 - kh : 2 - kh + rows, :], 1 - kw))
    return jnp.stack(pieces, axis=1).reshape(outs * 9, rows * cols)


def conv_back_stacked(stacked, weight, rows, cols):
    outs = weight.shape[0]
    inner = weight.shape[3]
    flat_w = weight.reshape(outs * 9, inner)
    result = lax.dot_general(
        flat_w, stacked, (((0,), (0,)), ((), ())), preferred_element_type=jnp.float32
    )
    return result.reshape(inner, rows, cols)


def filter_grad(grad_out, cols_in):
    outs, rows, cols = grad_out.shape
    result = lax.dot_general(
        grad_out.reshape(outs, rows * cols),
        cols_in,
        (((1,), (1,)), ((), ())),
        preferred_element_type=jnp.float32,
    )
    return result.reshape(outs, 3, 3, cols_in.shape[0] // 9)


def chan_sum_scatter(part, axis):
    count = lax.axis_size(axis)
    me = lax.axis_index(axis)
    blocks = part.reshape((count, part.shape[0] // count) + part.shape[1:])
    bit = 1
    while bit < count:
        pairs = blocks.reshape((blocks.shape[0] // 2, 2) + blocks.shape[1:])
        side = (me // bit) % 2
        keep = lax.dynamic_index_in_dim(pairs, side, axis=1, keepdims=False)
        send = lax.dynamic_index_in_dim(pairs, 1 - side, axis=1, keepdims=False)
        blocks = keep + lax.ppermute(send, axis, [(i, i ^ bit) for i in range(count)])
        bit *= 2
    return blocks.reshape(blocks.shape[1:])


def halving_sum(flat, axis, bits):
    me = lax.axis_index(axis)
    count = lax.axis_size(axis)
    for bit in bits:
        pairs = flat.reshape(2, flat.shape[0] // 2)
        side = (me >> bit) & 1
        keep = lax.dynamic_index_in_dim(pairs, side, axis=0, keepdims=False)
        send = lax.dynamic_index_in_dim(pairs, 1 - side, axis=0, keepdims=False)
        flat = keep + lax.ppermute(send, axis, [(i, i ^ (1 << bit)) for i in range(count)])
    return flat


def halving_gather(part, axis, bits):
    me = lax.axis_index(axis)
    count = lax.axis_size(axis)
    for bit in reversed(bits):
        got = lax.ppermute(part, axis, [(i, i ^ (1 << bit)) for i in range(count)])
        side = (me >> bit) & 1
        part = jnp.where(side == 0, jnp.concatenate([part, got]), jnp.concatenate([got, part]))
    return part


def chan_gather(block, axis):
    levels = lax.axis_size(axis).bit_length() - 1
    return halving_gather(block, axis, tuple(reversed(range(levels))))


def strip_allreduce(terms, axis):
    count = lax.axis_size(axis)
    levels = count.bit_length() - 1
    assert 1 << levels == count
    flat = jnp.concatenate([t.reshape(-1) for t in terms])
    half = flat.shape[0] // 2
    orders = (tuple(range(levels)), (1, 0) + tuple(range(2, levels)))
    outs = []
    for part, bits in zip((flat[:half], flat[half:]), orders):
        summed = halving_sum(part, axis, bits).astype(jnp.bfloat16)
        outs.append(halving_gather(summed, axis, bits))
    flat = jnp.concatenate(outs).astype(jnp.float32)
    results, at = [], 0
    for t in terms:
        results.append(flat[at : at + t.size].reshape(t.shape))
        at += t.size
    return results


def body(features, first_filters, second_filters, out_grad):
    blocks, rows, cols = features.shape
    dy_pad = extended(out_grad, (("strip", 1),), 1)
    dy_stack = back_stack(dy_pad)
    hidden_grad = chan_sum_scatter(
        conv_back_stacked(dy_stack, second_filters, rows, cols), "chan"
    )
    x_pad = extended(features, (("strip", 1),), 2)
    x_all = chan_gather(x_pad, "chan")
    x_cols = im2col(x_all)
    pre_wide = conv_fwd(x_cols, first_filters, rows + 2, cols)
    pre_full = pre_wide[:, 1 : rows + 1]
    pre = pre_full.astype(jnp.bfloat16)
    strip_at = lax.axis_index("strip")
    row_at = jnp.arange(rows + 2)[None, :, None]
    outside = ((row_at == 0) & (strip_at == 0)) | (
        (row_at == rows + 1) & (strip_at == lax.axis_size("strip") - 1)
    )
    h_pad = jnp.where(outside, 0.0, jax.nn.silu(pre_wide)).astype(jnp.bfloat16)
    h_all = chan_gather(h_pad, "chan")
    h_cols = im2col(h_all)
    (second_grad,) = strip_allreduce((filter_grad(out_grad, h_cols),), "strip")
    output = (features.astype(jnp.float32) + conv_fwd(h_cols, second_filters, rows, cols)).astype(jnp.bfloat16)
    pre_val = pre.astype(jnp.float32)
    sig = jax.nn.sigmoid(pre_val)
    pre_grad = (hidden_grad * sig * (1.0 + pre_val * (1.0 - sig))).astype(jnp.bfloat16)
    da_pad = extended(pre_grad, (("strip", 1),), 1)
    wide_grad = jnp.pad(pre_grad, ((0, 0), (1, 1), (0, 0)))
    (first_grad,) = strip_allreduce((filter_grad(wide_grad, x_cols),), "strip")
    da_stack = back_stack(da_pad)
    input_term = chan_sum_scatter(
        conv_back_stacked(da_stack, first_filters, rows, cols), "chan"
    )
    input_grad = (out_grad.astype(jnp.float32) + input_term).astype(jnp.bfloat16)
    return (output, input_grad, first_grad, second_grad)


def solution(mesh):
    in_specs = (
        P("chan", "strip", None),
        P("chan", None, None, None),
        P("chan", None, None, None),
        P("chan", "strip", None),
    )
    out_specs = (
        P("chan", "strip", None),
        P("chan", "strip", None),
        P("chan", None, None, None),
        P("chan", None, None, None),
    )
    return jax.shard_map(body, mesh=mesh, in_specs=in_specs, out_specs=out_specs, check_vma=False)
```

```python
import jax
import jax.numpy as jnp
from jax import lax
from jax.sharding import PartitionSpec as P


def extended(cells, sides, width):
    for axis, dim in sides:
        count = lax.axis_size(axis)
        ends = count - 1
        head = lax.slice_in_dim(cells, 0, width, axis=dim)
        tail = lax.slice_in_dim(cells, cells.shape[dim] - width, cells.shape[dim], axis=dim)
        cells = jnp.concatenate(
            [
                lax.ppermute(tail, axis, [(i, (i + 1) % count) for i in range(ends)]),
                cells,
                lax.ppermute(head, axis, [((i + 1) % count, i) for i in range(ends)]),
            ],
            axis=dim,
        )
    return cells


def take_cols(field, shift):
    if shift == 0:
        return field
    edge = jnp.zeros(field.shape[:-1] + (1,), field.dtype)
    if shift > 0:
        return jnp.concatenate([field[..., 1:], edge], axis=-1)
    return jnp.concatenate([edge, field[..., :-1]], axis=-1)


def im2col(padded):
    chans, rows_pad, cols = padded.shape
    rows = rows_pad - 2
    pieces = []
    for kh in range(3):
        for kw in range(3):
            pieces.append(take_cols(padded[:, kh : kh + rows, :], kw - 1))
    return jnp.stack(pieces, axis=0).reshape(9 * chans, rows * cols)


def conv_fwd(cols_in, weight, rows, cols):
    outs = weight.shape[0]
    flat_w = weight.reshape(outs, -1)
    total = jnp.dot(flat_w, cols_in, preferred_element_type=jnp.float32)
    return total.reshape(outs, rows, cols)


def back_stack(padded):
    outs, rows_pad, cols = padded.shape
    rows = rows_pad - 2
    pieces = []
    for kh in range(3):
        for kw in range(3):
            pieces.append(take_cols(padded[:, 2 - kh : 2 - kh + rows, :], 1 - kw))
    return jnp.stack(pieces, axis=1).reshape(outs * 9, rows * cols)


def conv_back_stacked(stacked, weight, rows, cols):
    outs = weight.shape[0]
    inner = weight.shape[3]
    flat_w = weight.reshape(outs * 9, inner)
    result = lax.dot_general(
        flat_w, stacked, (((0,), (0,)), ((), ())), preferred_element_type=jnp.float32
    )
    return result.reshape(inner, rows, cols)


def filter_grad(grad_out, cols_in):
    outs, rows, cols = grad_out.shape
    result = lax.dot_general(
        grad_out.reshape(outs, rows * cols),
        cols_in,
        (((1,), (1,)), ((), ())),
        preferred_element_type=jnp.float32,
    )
    return result.reshape(outs, 3, 3, cols_in.shape[0] // 9)


def chan_sum_scatter(part, axis):
    count = lax.axis_size(axis)
    me = lax.axis_index(axis)
    blocks = part.reshape((count, part.shape[0] // count) + part.shape[1:])
    bit = 1
    while bit < count:
        pairs = blocks.reshape((blocks.shape[0] // 2, 2) + blocks.shape[1:])
        side = (me // bit) % 2
        keep = lax.dynamic_index_in_dim(pairs, side, axis=1, keepdims=False)
        send = lax.dynamic_index_in_dim(pairs, 1 - side, axis=1, keepdims=False)
        blocks = keep + lax.ppermute(send, axis, [(i, i ^ bit) for i in range(count)])
        bit *= 2
    return blocks.reshape(blocks.shape[1:])


def halving_sum(flat, axis, bits):
    me = lax.axis_index(axis)
    count = lax.axis_size(axis)
    for bit in bits:
        pairs = flat.reshape(2, flat.shape[0] // 2)
        side = (me >> bit) & 1
        keep = lax.dynamic_index_in_dim(pairs, side, axis=0, keepdims=False)
        send = lax.dynamic_index_in_dim(pairs, 1 - side, axis=0, keepdims=False)
        flat = keep + lax.ppermute(send, axis, [(i, i ^ (1 << bit)) for i in range(count)])
    return flat


def halving_gather(part, axis, bits):
    me = lax.axis_index(axis)
    count = lax.axis_size(axis)
    for bit in reversed(bits):
        got = lax.ppermute(part, axis, [(i, i ^ (1 << bit)) for i in range(count)])
        side = (me >> bit) & 1
        part = jnp.where(side == 0, jnp.concatenate([part, got]), jnp.concatenate([got, part]))
    return part


def chan_gather(block, axis):
    levels = lax.axis_size(axis).bit_length() - 1
    return halving_gather(block, axis, tuple(reversed(range(levels))))


def strip_allreduce(terms, axis):
    count = lax.axis_size(axis)
    levels = count.bit_length() - 1
    assert 1 << levels == count
    flat = jnp.concatenate([t.reshape(-1) for t in terms])
    half = flat.shape[0] // 2
    orders = (tuple(range(levels)), (1, 0) + tuple(range(2, levels)))
    outs = []
    for part, bits in zip((flat[:half], flat[half:]), orders):
        summed = halving_sum(part, axis, bits).astype(jnp.bfloat16)
        outs.append(halving_gather(summed, axis, bits))
    flat = jnp.concatenate(outs).astype(jnp.float32)
    results, at = [], 0
    for t in terms:
        results.append(flat[at : at + t.size].reshape(t.shape))
        at += t.size
    return results


def body(features, first_filters, second_filters, out_grad):
    blocks, rows, cols = features.shape
    both_pad = extended(jnp.concatenate([features, out_grad]), (("strip", 1),), 1)
    x_pad, dy_pad = both_pad[:blocks], both_pad[blocks:]
    dy_stack = back_stack(dy_pad)
    hidden_grad = chan_sum_scatter(
        conv_back_stacked(dy_stack, second_filters, rows, cols), "chan"
    )
    x_all = chan_gather(x_pad, "chan")
    x_cols = im2col(x_all)
    pre_full = conv_fwd(x_cols, first_filters, rows, cols)
    pre = pre_full.astype(jnp.bfloat16)
    hidden = jax.nn.silu(pre_full).astype(jnp.bfloat16)
    h_pad = extended(hidden, (("strip", 1),), 1)
    h_all = chan_gather(h_pad, "chan")
    h_cols = im2col(h_all)
    (second_grad,) = strip_allreduce((filter_grad(out_grad, h_cols),), "strip")
    output = (features.astype(jnp.float32) + conv_fwd(h_cols, second_filters, rows, cols)).astype(jnp.bfloat16)
    pre_val = pre.astype(jnp.float32)
    sig = jax.nn.sigmoid(pre_val)
    pre_grad = (hidden_grad * sig * (1.0 + pre_val * (1.0 - sig))).astype(jnp.bfloat16)
    da_pad = extended(pre_grad, (("strip", 1),), 1)
    (first_grad,) = strip_allreduce((filter_grad(pre_grad, x_cols),), "strip")
    da_stack = back_stack(da_pad)
    input_term = chan_sum_scatter(
        conv_back_stacked(da_stack, first_filters, rows, cols), "chan"
    )
    input_grad = (out_grad.astype(jnp.float32) + input_term).astype(jnp.bfloat16)
    return (output, input_grad, first_grad, second_grad)


def solution(mesh):
    in_specs = (
        P("chan", "strip", None),
        P("chan", None, None, None),
        P("chan", None, None, None),
        P("chan", "strip", None),
    )
    out_specs = (
        P("chan", "strip", None),
        P("chan", "strip", None),
        P("chan", None, None, None),
        P("chan", None, None, None),
    )
    return jax.shard_map(body, mesh=mesh, in_specs=in_specs, out_specs=out_specs, check_vma=False)
```

```python
import jax
import jax.numpy as jnp
from jax import lax
from jax.sharding import PartitionSpec as P


def extended(cells, sides, width):
    for axis, dim in sides:
        count = lax.axis_size(axis)
        ends = count - 1
        head = lax.slice_in_dim(cells, 0, width, axis=dim)
        tail = lax.slice_in_dim(cells, cells.shape[dim] - width, cells.shape[dim], axis=dim)
        cells = jnp.concatenate(
            [
                lax.ppermute(tail, axis, [(i, (i + 1) % count) for i in range(ends)]),
                cells,
                lax.ppermute(head, axis, [((i + 1) % count, i) for i in range(ends)]),
            ],
            axis=dim,
        )
    return cells


def take_cols(field, shift):
    if shift == 0:
        return field
    edge = jnp.zeros(field.shape[:-1] + (1,), field.dtype)
    if shift > 0:
        return jnp.concatenate([field[..., 1:], edge], axis=-1)
    return jnp.concatenate([edge, field[..., :-1]], axis=-1)


def im2col(padded):
    chans, rows_pad, cols = padded.shape
    rows = rows_pad - 2
    pieces = []
    for kh in range(3):
        for kw in range(3):
            pieces.append(take_cols(padded[:, kh : kh + rows, :], kw - 1))
    return jnp.stack(pieces, axis=0).reshape(9 * chans, rows * cols)


def conv_fwd(cols_in, weight, rows, cols):
    outs = weight.shape[0]
    flat_w = weight.reshape(outs, -1)
    total = jnp.dot(flat_w, cols_in, preferred_element_type=jnp.float32)
    return total.reshape(outs, rows, cols)


def back_stack(padded):
    outs, rows_pad, cols = padded.shape
    rows = rows_pad - 2
    pieces = []
    for kh in range(3):
        for kw in range(3):
            pieces.append(take_cols(padded[:, 2 - kh : 2 - kh + rows, :], 1 - kw))
    return jnp.stack(pieces, axis=1).reshape(outs * 9, rows * cols)


def conv_back_stacked(stacked, weight, rows, cols):
    outs = weight.shape[0]
    inner = weight.shape[3]
    flat_w = weight.reshape(outs * 9, inner)
    result = lax.dot_general(
        flat_w, stacked, (((0,), (0,)), ((), ())), preferred_element_type=jnp.float32
    )
    return result.reshape(inner, rows, cols)


def filter_grad(grad_out, cols_in):
    outs, rows, cols = grad_out.shape
    result = lax.dot_general(
        grad_out.reshape(outs, rows * cols),
        cols_in,
        (((1,), (1,)), ((), ())),
        preferred_element_type=jnp.float32,
    )
    return result.reshape(outs, 3, 3, cols_in.shape[0] // 9)


def chan_sum_scatter(part, axis):
    count = lax.axis_size(axis)
    me = lax.axis_index(axis)
    blocks = part.reshape((count, part.shape[0] // count) + part.shape[1:])
    bit = 1
    while bit < count:
        pairs = blocks.reshape((blocks.shape[0] // 2, 2) + blocks.shape[1:])
        side = (me // bit) % 2
        keep = lax.dynamic_index_in_dim(pairs, side, axis=1, keepdims=False)
        send = lax.dynamic_index_in_dim(pairs, 1 - side, axis=1, keepdims=False)
        blocks = keep + lax.ppermute(send, axis, [(i, i ^ bit) for i in range(count)])
        bit *= 2
    return blocks.reshape(blocks.shape[1:])


def halving_sum(flat, axis, bits):
    me = lax.axis_index(axis)
    count = lax.axis_size(axis)
    for bit in bits:
        pairs = flat.reshape(2, flat.shape[0] // 2)
        side = (me >> bit) & 1
        keep = lax.dynamic_index_in_dim(pairs, side, axis=0, keepdims=False)
        send = lax.dynamic_index_in_dim(pairs, 1 - side, axis=0, keepdims=False)
        flat = keep + lax.ppermute(send, axis, [(i, i ^ (1 << bit)) for i in range(count)])
    return flat


def halving_gather(part, axis, bits):
    me = lax.axis_index(axis)
    count = lax.axis_size(axis)
    for bit in reversed(bits):
        got = lax.ppermute(part, axis, [(i, i ^ (1 << bit)) for i in range(count)])
        side = (me >> bit) & 1
        part = jnp.where(side == 0, jnp.concatenate([part, got]), jnp.concatenate([got, part]))
    return part


def chan_gather(block, axis):
    levels = lax.axis_size(axis).bit_length() - 1
    return halving_gather(block, axis, tuple(reversed(range(levels))))


def strip_allreduce(term, axis, swap):
    count = lax.axis_size(axis)
    levels = count.bit_length() - 1
    assert 1 << levels == count
    bits = tuple(range(levels))
    if swap:
        bits = (1, 0) + bits[2:]
    summed = halving_sum(term.reshape(-1), axis, bits).astype(jnp.bfloat16)
    return halving_gather(summed, axis, bits).astype(jnp.float32).reshape(term.shape)


def body(features, first_filters, second_filters, out_grad):
    blocks, rows, cols = features.shape
    both_pad = extended(jnp.concatenate([features, out_grad]), (("strip", 1),), 1)
    x_pad, dy_pad = both_pad[:blocks], both_pad[blocks:]
    dy_stack = back_stack(dy_pad)
    hidden_grad = chan_sum_scatter(
        conv_back_stacked(dy_stack, second_filters, rows, cols), "chan"
    )
    x_all = chan_gather(x_pad, "chan")
    x_cols = im2col(x_all)
    pre_full = conv_fwd(x_cols, first_filters, rows, cols)
    pre = pre_full.astype(jnp.bfloat16)
    hidden = jax.nn.silu(pre_full).astype(jnp.bfloat16)
    h_pad = extended(hidden, (("strip", 1),), 1)
    h_all = chan_gather(h_pad, "chan")
    h_cols = im2col(h_all)
    second_grad = strip_allreduce(filter_grad(out_grad, h_cols), "strip", False)
    output = (features.astype(jnp.float32) + conv_fwd(h_cols, second_filters, rows, cols)).astype(jnp.bfloat16)
    pre_val = pre.astype(jnp.float32)
    sig = jax.nn.sigmoid(pre_val)
    pre_grad = (hidden_grad * sig * (1.0 + pre_val * (1.0 - sig))).astype(jnp.bfloat16)
    da_pad = extended(pre_grad, (("strip", 1),), 1)
    first_grad = strip_allreduce(filter_grad(pre_grad, x_cols), "strip", True)
    da_stack = back_stack(da_pad)
    input_term = chan_sum_scatter(
        conv_back_stacked(da_stack, first_filters, rows, cols), "chan"
    )
    input_grad = (out_grad.astype(jnp.float32) + input_term).astype(jnp.bfloat16)
    return (output, input_grad, first_grad, second_grad)


def solution(mesh):
    in_specs = (
        P("chan", "strip", None),
        P("chan", None, None, None),
        P("chan", None, None, None),
        P("chan", "strip", None),
    )
    out_specs = (
        P("chan", "strip", None),
        P("chan", "strip", None),
        P("chan", None, None, None),
        P("chan", None, None, None),
    )
    return jax.shard_map(body, mesh=mesh, in_specs=in_specs, out_specs=out_specs, check_vma=False)
```

```python
import jax
import jax.numpy as jnp
from jax import lax
from jax.sharding import PartitionSpec as P


def extended(cells, sides, width):
    for axis, dim in sides:
        count = lax.axis_size(axis)
        ends = count - 1
        head = lax.slice_in_dim(cells, 0, width, axis=dim)
        tail = lax.slice_in_dim(cells, cells.shape[dim] - width, cells.shape[dim], axis=dim)
        cells = jnp.concatenate(
            [
                lax.ppermute(tail, axis, [(i, (i + 1) % count) for i in range(ends)]),
                cells,
                lax.ppermute(head, axis, [((i + 1) % count, i) for i in range(ends)]),
            ],
            axis=dim,
        )
    return cells


def take_cols(field, shift):
    if shift == 0:
        return field
    edge = jnp.zeros(field.shape[:-1] + (1,), field.dtype)
    if shift > 0:
        return jnp.concatenate([field[..., 1:], edge], axis=-1)
    return jnp.concatenate([edge, field[..., :-1]], axis=-1)


def im2col(padded):
    chans, rows_pad, cols = padded.shape
    rows = rows_pad - 2
    pieces = []
    for kh in range(3):
        for kw in range(3):
            pieces.append(take_cols(padded[:, kh : kh + rows, :], kw - 1))
    return jnp.stack(pieces, axis=0).reshape(9 * chans, rows * cols)


def conv_fwd(cols_in, weight, rows, cols):
    outs = weight.shape[0]
    flat_w = weight.reshape(outs, -1)
    total = jnp.dot(flat_w, cols_in, preferred_element_type=jnp.float32)
    return total.reshape(outs, rows, cols)


def back_stack(padded):
    outs, rows_pad, cols = padded.shape
    rows = rows_pad - 2
    pieces = []
    for kh in range(3):
        for kw in range(3):
            pieces.append(take_cols(padded[:, 2 - kh : 2 - kh + rows, :], 1 - kw))
    return jnp.stack(pieces, axis=1).reshape(outs * 9, rows * cols)


def conv_back_stacked(stacked, weight, rows, cols):
    outs = weight.shape[0]
    inner = weight.shape[3]
    flat_w = weight.reshape(outs * 9, inner)
    result = lax.dot_general(
        flat_w, stacked, (((0,), (0,)), ((), ())), preferred_element_type=jnp.float32
    )
    return result.reshape(inner, rows, cols)


def filter_grad(grad_out, cols_in):
    outs, rows, cols = grad_out.shape
    result = lax.dot_general(
        grad_out.reshape(outs, rows * cols),
        cols_in,
        (((1,), (1,)), ((), ())),
        preferred_element_type=jnp.float32,
    )
    return result.reshape(outs, 3, 3, cols_in.shape[0] // 9)


def chan_sum_scatter(part, axis):
    count = lax.axis_size(axis)
    me = lax.axis_index(axis)
    blocks = part.reshape((count, part.shape[0] // count) + part.shape[1:])
    bit = 1
    while bit < count:
        pairs = blocks.reshape((blocks.shape[0] // 2, 2) + blocks.shape[1:])
        side = (me // bit) % 2
        keep = lax.dynamic_index_in_dim(pairs, side, axis=1, keepdims=False)
        send = lax.dynamic_index_in_dim(pairs, 1 - side, axis=1, keepdims=False)
        blocks = keep + lax.ppermute(send, axis, [(i, i ^ bit) for i in range(count)])
        bit *= 2
    return blocks.reshape(blocks.shape[1:])


def halving_sum(flat, axis, bits):
    me = lax.axis_index(axis)
    count = lax.axis_size(axis)
    for bit in bits:
        pairs = flat.reshape(2, flat.shape[0] // 2)
        side = (me >> bit) & 1
        keep = lax.dynamic_index_in_dim(pairs, side, axis=0, keepdims=False)
        send = lax.dynamic_index_in_dim(pairs, 1 - side, axis=0, keepdims=False)
        flat = keep + lax.ppermute(send, axis, [(i, i ^ (1 << bit)) for i in range(count)])
    return flat


def halving_gather(part, axis, bits):
    me = lax.axis_index(axis)
    count = lax.axis_size(axis)
    for bit in reversed(bits):
        got = lax.ppermute(part, axis, [(i, i ^ (1 << bit)) for i in range(count)])
        side = (me >> bit) & 1
        part = jnp.where(side == 0, jnp.concatenate([part, got]), jnp.concatenate([got, part]))
    return part


def chan_gather(block, axis):
    levels = lax.axis_size(axis).bit_length() - 1
    return halving_gather(block, axis, tuple(reversed(range(levels))))


def strip_sum_parts(term, axis):
    count = lax.axis_size(axis)
    levels = count.bit_length() - 1
    assert 1 << levels == count
    flat = term.reshape(-1)
    half = flat.shape[0] // 2
    orders = (tuple(range(levels)), (1, 0) + tuple(range(2, levels)))
    return [
        halving_sum(part, axis, bits).astype(jnp.bfloat16)
        for part, bits in zip((flat[:half], flat[half:]), orders)
    ]


def strip_gather_parts(parts, axis, shape):
    count = lax.axis_size(axis)
    levels = count.bit_length() - 1
    orders = (tuple(range(levels)), (1, 0) + tuple(range(2, levels)))
    outs = [halving_gather(part, axis, bits) for part, bits in zip(parts, orders)]
    return jnp.concatenate(outs).astype(jnp.float32).reshape(shape)


def strip_allreduce(term, axis):
    return strip_gather_parts(strip_sum_parts(term, axis), axis, term.shape)


def body(features, first_filters, second_filters, out_grad):
    blocks, rows, cols = features.shape
    both_pad = extended(jnp.concatenate([features, out_grad]), (("strip", 1),), 1)
    x_pad, dy_pad = both_pad[:blocks], both_pad[blocks:]
    dy_stack = back_stack(dy_pad)
    hidden_grad = chan_sum_scatter(
        conv_back_stacked(dy_stack, second_filters, rows, cols), "chan"
    )
    x_all = chan_gather(x_pad, "chan")
    x_cols = im2col(x_all)
    pre_full = conv_fwd(x_cols, first_filters, rows, cols)
    pre = pre_full.astype(jnp.bfloat16)
    hidden = jax.nn.silu(pre_full).astype(jnp.bfloat16)
    pre_val = pre.astype(jnp.float32)
    sig = jax.nn.sigmoid(pre_val)
    pre_grad = (hidden_grad * sig * (1.0 + pre_val * (1.0 - sig))).astype(jnp.bfloat16)
    first_part = filter_grad(pre_grad, x_cols)
    h_pad = extended(hidden, (("strip", 1),), 1)
    first_sums = strip_sum_parts(first_part, "strip")
    h_all = chan_gather(h_pad, "chan")
    first_sums, h_all = lax.optimization_barrier((first_sums, h_all))
    first_grad = strip_gather_parts(first_sums, "strip", first_part.shape)
    h_cols = im2col(h_all)
    second_grad = strip_allreduce(filter_grad(out_grad, h_cols), "strip")
    output = (features.astype(jnp.float32) + conv_fwd(h_cols, second_filters, rows, cols)).astype(jnp.bfloat16)
    da_pad = extended(pre_grad, (("strip", 1),), 1)
    da_stack = back_stack(da_pad)
    input_term = chan_sum_scatter(
        conv_back_stacked(da_stack, first_filters, rows, cols), "chan"
    )
    input_grad = (out_grad.astype(jnp.float32) + input_term).astype(jnp.bfloat16)
    return (output, input_grad, first_grad, second_grad)


def solution(mesh):
    in_specs = (
        P("chan", "strip", None),
        P("chan", None, None, None),
        P("chan", None, None, None),
        P("chan", "strip", None),
    )
    out_specs = (
        P("chan", "strip", None),
        P("chan", "strip", None),
        P("chan", None, None, None),
        P("chan", None, None, None),
    )
    return jax.shard_map(body, mesh=mesh, in_specs=in_specs, out_specs=out_specs, check_vma=False)
```

```python
import jax
import jax.numpy as jnp
from jax import lax
from jax.sharding import PartitionSpec as P


def extended(cells, sides, width):
    for axis, dim in sides:
        count = lax.axis_size(axis)
        ends = count - 1
        head = lax.slice_in_dim(cells, 0, width, axis=dim)
        tail = lax.slice_in_dim(cells, cells.shape[dim] - width, cells.shape[dim], axis=dim)
        cells = jnp.concatenate(
            [
                lax.ppermute(tail, axis, [(i, (i + 1) % count) for i in range(ends)]),
                cells,
                lax.ppermute(head, axis, [((i + 1) % count, i) for i in range(ends)]),
            ],
            axis=dim,
        )
    return cells


def take_cols(field, shift):
    if shift == 0:
        return field
    edge = jnp.zeros(field.shape[:-1] + (1,), field.dtype)
    if shift > 0:
        return jnp.concatenate([field[..., 1:], edge], axis=-1)
    return jnp.concatenate([edge, field[..., :-1]], axis=-1)


def im2col(padded):
    chans, rows_pad, cols = padded.shape
    rows = rows_pad - 2
    pieces = []
    for kh in range(3):
        for kw in range(3):
            pieces.append(take_cols(padded[:, kh : kh + rows, :], kw - 1))
    return jnp.stack(pieces, axis=0).reshape(9 * chans, rows * cols)


def conv_fwd(cols_in, weight, rows, cols):
    outs = weight.shape[0]
    flat_w = weight.reshape(outs, -1)
    total = jnp.dot(flat_w, cols_in, preferred_element_type=jnp.float32)
    return total.reshape(outs, rows, cols)


def back_stack(padded):
    outs, rows_pad, cols = padded.shape
    rows = rows_pad - 2
    pieces = []
    for kh in range(3):
        for kw in range(3):
            pieces.append(take_cols(padded[:, 2 - kh : 2 - kh + rows, :], 1 - kw))
    return jnp.stack(pieces, axis=1).reshape(outs * 9, rows * cols)


def conv_back_stacked(stacked, weight, rows, cols):
    outs = weight.shape[0]
    inner = weight.shape[3]
    flat_w = weight.reshape(outs * 9, inner)
    result = lax.dot_general(
        flat_w, stacked, (((0,), (0,)), ((), ())), preferred_element_type=jnp.float32
    )
    return result.reshape(inner, rows, cols)


def filter_grad(grad_out, cols_in):
    outs, rows, cols = grad_out.shape
    result = lax.dot_general(
        grad_out.reshape(outs, rows * cols),
        cols_in,
        (((1,), (1,)), ((), ())),
        preferred_element_type=jnp.float32,
    )
    return result.reshape(outs, 3, 3, cols_in.shape[0] // 9)


def chan_sum_scatter(part, axis):
    count = lax.axis_size(axis)
    me = lax.axis_index(axis)
    blocks = part.reshape((count, part.shape[0] // count) + part.shape[1:])
    bit = 1
    while bit < count:
        pairs = blocks.reshape((blocks.shape[0] // 2, 2) + blocks.shape[1:])
        side = (me // bit) % 2
        keep = lax.dynamic_index_in_dim(pairs, side, axis=1, keepdims=False)
        send = lax.dynamic_index_in_dim(pairs, 1 - side, axis=1, keepdims=False)
        blocks = keep + lax.ppermute(send, axis, [(i, i ^ bit) for i in range(count)])
        bit *= 2
    return blocks.reshape(blocks.shape[1:])


def halving_sum(flat, axis, bits):
    me = lax.axis_index(axis)
    count = lax.axis_size(axis)
    for bit in bits:
        pairs = flat.reshape(2, flat.shape[0] // 2)
        side = (me >> bit) & 1
        keep = lax.dynamic_index_in_dim(pairs, side, axis=0, keepdims=False)
        send = lax.dynamic_index_in_dim(pairs, 1 - side, axis=0, keepdims=False)
        flat = keep + lax.ppermute(send, axis, [(i, i ^ (1 << bit)) for i in range(count)])
    return flat


def halving_gather(part, axis, bits):
    me = lax.axis_index(axis)
    count = lax.axis_size(axis)
    for bit in reversed(bits):
        got = lax.ppermute(part, axis, [(i, i ^ (1 << bit)) for i in range(count)])
        side = (me >> bit) & 1
        offset = (side * part.shape[0],) + (0,) * (part.ndim - 1)
        part = lax.dynamic_update_slice(jnp.concatenate([got, got]), part, offset)
    return part


def chan_gather(block, axis):
    levels = lax.axis_size(axis).bit_length() - 1
    return halving_gather(block, axis, tuple(reversed(range(levels))))


def strip_allreduce(terms, axis):
    count = lax.axis_size(axis)
    levels = count.bit_length() - 1
    assert 1 << levels == count
    flat = jnp.concatenate([t.reshape(-1) for t in terms])
    half = flat.shape[0] // 2
    orders = (tuple(range(levels)), (1, 0) + tuple(range(2, levels)))
    outs = []
    for part, bits in zip((flat[:half], flat[half:]), orders):
        summed = halving_sum(part, axis, bits).astype(jnp.bfloat16)
        outs.append(halving_gather(summed, axis, bits))
    flat = jnp.concatenate(outs).astype(jnp.float32)
    results, at = [], 0
    for t in terms:
        results.append(flat[at : at + t.size].reshape(t.shape))
        at += t.size
    return results


def body(features, first_filters, second_filters, out_grad):
    blocks, rows, cols = features.shape
    both_pad = extended(jnp.concatenate([features, out_grad]), (("strip", 1),), 1)
    x_pad, dy_pad = both_pad[:blocks], both_pad[blocks:]
    dy_stack = back_stack(dy_pad)
    hidden_grad = chan_sum_scatter(
        conv_back_stacked(dy_stack, second_filters, rows, cols), "chan"
    )
    x_all = chan_gather(x_pad, "chan")
    x_cols = im2col(x_all)
    pre_full = conv_fwd(x_cols, first_filters, rows, cols)
    pre = pre_full.astype(jnp.bfloat16)
    hidden = jax.nn.silu(pre_full).astype(jnp.bfloat16)
    h_pad = extended(hidden, (("strip", 1),), 1)
    h_all = chan_gather(h_pad, "chan")
    h_cols = im2col(h_all)
    (second_grad,) = strip_allreduce((filter_grad(out_grad, h_cols),), "strip")
    output = (features.astype(jnp.float32) + conv_fwd(h_cols, second_filters, rows, cols)).astype(jnp.bfloat16)
    pre_val = pre.astype(jnp.float32)
    sig = jax.nn.sigmoid(pre_val)
    pre_grad = (hidden_grad * sig * (1.0 + pre_val * (1.0 - sig))).astype(jnp.bfloat16)
    da_pad = extended(pre_grad, (("strip", 1),), 1)
    (first_grad,) = strip_allreduce((filter_grad(pre_grad, x_cols),), "strip")
    da_stack = back_stack(da_pad)
    input_term = chan_sum_scatter(
        conv_back_stacked(da_stack, first_filters, rows, cols), "chan"
    )
    input_grad = (out_grad.astype(jnp.float32) + input_term).astype(jnp.bfloat16)
    return (output, input_grad, first_grad, second_grad)


def solution(mesh):
    in_specs = (
        P("chan", "strip", None),
        P("chan", None, None, None),
        P("chan", None, None, None),
        P("chan", "strip", None),
    )
    out_specs = (
        P("chan", "strip", None),
        P("chan", "strip", None),
        P("chan", None, None, None),
        P("chan", None, None, None),
    )
    return jax.shard_map(body, mesh=mesh, in_specs=in_specs, out_specs=out_specs, check_vma=False)
```

```python
import jax
import jax.numpy as jnp
from jax import lax
from jax.sharding import PartitionSpec as P


def extended(cells, sides, width):
    for axis, dim in sides:
        count = lax.axis_size(axis)
        ends = count - 1
        head = lax.slice_in_dim(cells, 0, width, axis=dim)
        tail = lax.slice_in_dim(cells, cells.shape[dim] - width, cells.shape[dim], axis=dim)
        cells = jnp.concatenate(
            [
                lax.ppermute(tail, axis, [(i, (i + 1) % count) for i in range(ends)]),
                cells,
                lax.ppermute(head, axis, [((i + 1) % count, i) for i in range(ends)]),
            ],
            axis=dim,
        )
    return cells


def take_cols(field, shift):
    if shift == 0:
        return field
    edge = jnp.zeros(field.shape[:-1] + (1,), field.dtype)
    if shift > 0:
        return jnp.concatenate([field[..., 1:], edge], axis=-1)
    return jnp.concatenate([edge, field[..., :-1]], axis=-1)


def im2col(padded):
    chans, rows_pad, cols = padded.shape
    rows = rows_pad - 2
    pieces = []
    for kh in range(3):
        for kw in range(3):
            pieces.append(take_cols(padded[:, kh : kh + rows, :], kw - 1))
    return jnp.stack(pieces, axis=0).reshape(9 * chans, rows * cols)


def conv_fwd(cols_in, weight, rows, cols):
    outs = weight.shape[0]
    flat_w = weight.reshape(outs, -1)
    total = jnp.dot(flat_w, cols_in, preferred_element_type=jnp.float32)
    return total.reshape(outs, rows, cols)


def back_stack(padded):
    outs, rows_pad, cols = padded.shape
    rows = rows_pad - 2
    pieces = []
    for kh in range(3):
        for kw in range(3):
            pieces.append(take_cols(padded[:, 2 - kh : 2 - kh + rows, :], 1 - kw))
    return jnp.stack(pieces, axis=1).reshape(outs * 9, rows * cols)


def conv_back_stacked(stacked, weight, rows, cols):
    outs = weight.shape[0]
    inner = weight.shape[3]
    flat_w = weight.reshape(outs * 9, inner)
    result = lax.dot_general(
        flat_w, stacked, (((0,), (0,)), ((), ())), preferred_element_type=jnp.float32
    )
    return result.reshape(inner, rows, cols)


def filter_grad(grad_out, cols_in):
    outs, rows, cols = grad_out.shape
    result = lax.dot_general(
        grad_out.reshape(outs, rows * cols),
        cols_in,
        (((1,), (1,)), ((), ())),
        preferred_element_type=jnp.float32,
    )
    return result.reshape(outs, 3, 3, cols_in.shape[0] // 9)


def chan_sum_scatter(part, axis):
    count = lax.axis_size(axis)
    me = lax.axis_index(axis)
    blocks = part.reshape((count, part.shape[0] // count) + part.shape[1:])
    bit = 1
    while bit < count:
        pairs = blocks.reshape((blocks.shape[0] // 2, 2) + blocks.shape[1:])
        side = (me // bit) % 2
        keep = lax.dynamic_index_in_dim(pairs, side, axis=1, keepdims=False)
        send = lax.dynamic_index_in_dim(pairs, 1 - side, axis=1, keepdims=False)
        blocks = keep + lax.ppermute(send, axis, [(i, i ^ bit) for i in range(count)])
        bit *= 2
    return blocks.reshape(blocks.shape[1:])


def halving_sum(flat, axis, bits):
    me = lax.axis_index(axis)
    count = lax.axis_size(axis)
    for bit in bits:
        pairs = flat.reshape(2, flat.shape[0] // 2)
        side = (me >> bit) & 1
        keep = lax.dynamic_index_in_dim(pairs, side, axis=0, keepdims=False)
        send = lax.dynamic_index_in_dim(pairs, 1 - side, axis=0, keepdims=False)
        flat = keep + lax.ppermute(send, axis, [(i, i ^ (1 << bit)) for i in range(count)])
    return flat


def halving_gather(part, axis, bits):
    me = lax.axis_index(axis)
    count = lax.axis_size(axis)
    for bit in reversed(bits):
        got = lax.ppermute(part, axis, [(i, i ^ (1 << bit)) for i in range(count)])
        side = (me >> bit) & 1
        part = jnp.where(side == 0, jnp.concatenate([part, got]), jnp.concatenate([got, part]))
    return part


def chan_gather(block, axis):
    count = lax.axis_size(axis)
    levels = count.bit_length() - 1
    whole = halving_gather(block, axis, (0,) + tuple(range(levels - 1, 0, -1)))
    whole = whole.reshape((2, count // 2) + block.shape).swapaxes(0, 1)
    return whole.reshape((count * block.shape[0],) + block.shape[1:])


def strip_allreduce(terms, axis):
    count = lax.axis_size(axis)
    levels = count.bit_length() - 1
    assert 1 << levels == count
    flat = jnp.concatenate([t.reshape(-1) for t in terms])
    half = flat.shape[0] // 2
    orders = (tuple(range(levels)), (1, 0) + tuple(range(2, levels)))
    outs = []
    for part, bits in zip((flat[:half], flat[half:]), orders):
        summed = halving_sum(part, axis, bits).astype(jnp.bfloat16)
        outs.append(halving_gather(summed, axis, bits))
    flat = jnp.concatenate(outs).astype(jnp.float32)
    results, at = [], 0
    for t in terms:
        results.append(flat[at : at + t.size].reshape(t.shape))
        at += t.size
    return results


def body(features, first_filters, second_filters, out_grad):
    blocks, rows, cols = features.shape
    both_pad = extended(jnp.concatenate([features, out_grad]), (("strip", 1),), 1)
    x_pad, dy_pad = both_pad[:blocks], both_pad[blocks:]
    dy_stack = back_stack(dy_pad)
    hidden_grad = chan_sum_scatter(
        conv_back_stacked(dy_stack, second_filters, rows, cols), "chan"
    )
    x_all = chan_gather(x_pad, "chan")
    x_cols = im2col(x_all)
    pre_full = conv_fwd(x_cols, first_filters, rows, cols)
    pre = pre_full.astype(jnp.bfloat16)
    hidden = jax.nn.silu(pre_full).astype(jnp.bfloat16)
    h_pad = extended(hidden, (("strip", 1),), 1)
    h_all = chan_gather(h_pad, "chan")
    h_cols = im2col(h_all)
    (second_grad,) = strip_allreduce((filter_grad(out_grad, h_cols),), "strip")
    output = (features.astype(jnp.float32) + conv_fwd(h_cols, second_filters, rows, cols)).astype(jnp.bfloat16)
    pre_val = pre.astype(jnp.float32)
    sig = jax.nn.sigmoid(pre_val)
    pre_grad = (hidden_grad * sig * (1.0 + pre_val * (1.0 - sig))).astype(jnp.bfloat16)
    da_pad = extended(pre_grad, (("strip", 1),), 1)
    (first_grad,) = strip_allreduce((filter_grad(pre_grad, x_cols),), "strip")
    da_stack = back_stack(da_pad)
    input_term = chan_sum_scatter(
        conv_back_stacked(da_stack, first_filters, rows, cols), "chan"
    )
    input_grad = (out_grad.astype(jnp.float32) + input_term).astype(jnp.bfloat16)
    return (output, input_grad, first_grad, second_grad)


def solution(mesh):
    in_specs = (
        P("chan", "strip", None),
        P("chan", None, None, None),
        P("chan", None, None, None),
        P("chan", "strip", None),
    )
    out_specs = (
        P("chan", "strip", None),
        P("chan", "strip", None),
        P("chan", None, None, None),
        P("chan", None, None, None),
    )
    return jax.shard_map(body, mesh=mesh, in_specs=in_specs, out_specs=out_specs, check_vma=False)
```

```python
import jax
import jax.numpy as jnp
from jax import lax
from jax.sharding import PartitionSpec as P


def extended(cells, sides, width):
    for axis, dim in sides:
        count = lax.axis_size(axis)
        ends = count - 1
        head = lax.slice_in_dim(cells, 0, width, axis=dim)
        tail = lax.slice_in_dim(cells, cells.shape[dim] - width, cells.shape[dim], axis=dim)
        cells = jnp.concatenate(
            [
                lax.ppermute(tail, axis, [(i, (i + 1) % count) for i in range(ends)]),
                cells,
                lax.ppermute(head, axis, [((i + 1) % count, i) for i in range(ends)]),
            ],
            axis=dim,
        )
    return cells


def take_cols(field, shift):
    if shift == 0:
        return field
    edge = jnp.zeros(field.shape[:-1] + (1,), field.dtype)
    if shift > 0:
        return jnp.concatenate([field[..., 1:], edge], axis=-1)
    return jnp.concatenate([edge, field[..., :-1]], axis=-1)


def im2col(padded):
    chans, rows_pad, cols = padded.shape
    rows = rows_pad - 2
    pieces = []
    for kh in range(3):
        for kw in range(3):
            pieces.append(take_cols(padded[:, kh : kh + rows, :], kw - 1))
    return jnp.stack(pieces, axis=0).reshape(9 * chans, rows * cols)


def conv_fwd(cols_in, weight, rows, cols):
    outs = weight.shape[0]
    flat_w = weight.reshape(outs, -1)
    total = jnp.dot(flat_w, cols_in, preferred_element_type=jnp.float32)
    return total.reshape(outs, rows, cols)


def back_stack(padded):
    outs, rows_pad, cols = padded.shape
    rows = rows_pad - 2
    pieces = []
    for kh in range(3):
        for kw in range(3):
            pieces.append(take_cols(padded[:, 2 - kh : 2 - kh + rows, :], 1 - kw))
    return jnp.stack(pieces, axis=1).reshape(outs * 9, rows * cols)


def conv_back_stacked(stacked, weight, rows, cols):
    outs = weight.shape[0]
    inner = weight.shape[3]
    flat_w = weight.reshape(outs * 9, inner)
    result = lax.dot_general(
        flat_w, stacked, (((0,), (0,)), ((), ())), preferred_element_type=jnp.float32
    )
    return result.reshape(inner, rows, cols)


def filter_grad(grad_out, cols_in):
    outs, rows, cols = grad_out.shape
    result = lax.dot_general(
        grad_out.reshape(outs, rows * cols),
        cols_in,
        (((1,), (1,)), ((), ())),
        preferred_element_type=jnp.float32,
    )
    return result.reshape(outs, 3, 3, cols_in.shape[0] // 9)


def chan_sum_scatter(part, axis):
    count = lax.axis_size(axis)
    me = lax.axis_index(axis)
    blocks = part.reshape((count, part.shape[0] // count) + part.shape[1:])
    bit = 1
    while bit < count:
        pairs = blocks.reshape((blocks.shape[0] // 2, 2) + blocks.shape[1:])
        side = (me // bit) % 2
        keep = lax.dynamic_index_in_dim(pairs, side, axis=1, keepdims=False)
        send = lax.dynamic_index_in_dim(pairs, 1 - side, axis=1, keepdims=False)
        blocks = keep + lax.ppermute(send, axis, [(i, i ^ bit) for i in range(count)])
        bit *= 2
    return blocks.reshape(blocks.shape[1:])


def halving_sum(flat, axis, bits):
    me = lax.axis_index(axis)
    count = lax.axis_size(axis)
    for bit in bits:
        pairs = flat.reshape(2, flat.shape[0] // 2)
        side = (me >> bit) & 1
        keep = lax.dynamic_index_in_dim(pairs, side, axis=0, keepdims=False)
        send = lax.dynamic_index_in_dim(pairs, 1 - side, axis=0, keepdims=False)
        flat = keep + lax.ppermute(send, axis, [(i, i ^ (1 << bit)) for i in range(count)])
    return flat


def halving_gather(part, axis, bits):
    me = lax.axis_index(axis)
    count = lax.axis_size(axis)
    for bit in reversed(bits):
        got = lax.ppermute(part, axis, [(i, i ^ (1 << bit)) for i in range(count)])
        side = (me >> bit) & 1
        part = jnp.where(side == 0, jnp.concatenate([part, got]), jnp.concatenate([got, part]))
    return part


def chan_gather(block, axis):
    levels = lax.axis_size(axis).bit_length() - 1
    return halving_gather(block, axis, tuple(reversed(range(levels))))


def strip_allreduce(terms, axis):
    count = lax.axis_size(axis)
    levels = count.bit_length() - 1
    assert 1 << levels == count
    flat = jnp.concatenate([t.reshape(-1) for t in terms])
    half = flat.shape[0] // 2
    orders = (tuple(range(levels)), (1, 0) + tuple(range(2, levels)))
    outs = []
    for part, bits in zip((flat[:half], flat[half:]), orders):
        summed = halving_sum(part, axis, bits).astype(jnp.bfloat16)
        outs.append(halving_gather(summed, axis, bits))
    flat = jnp.concatenate(outs).astype(jnp.float32)
    results, at = [], 0
    for t in terms:
        results.append(flat[at : at + t.size].reshape(t.shape))
        at += t.size
    return results


def body(features, first_filters, second_filters, out_grad):
    blocks, rows, cols = features.shape
    both_pad = extended(jnp.concatenate([features, out_grad]), (("strip", 1),), 1)
    x_pad, dy_pad = both_pad[:blocks], both_pad[blocks:]
    dy_stack = back_stack(dy_pad)
    hidden_grad = chan_sum_scatter(
        conv_back_stacked(dy_stack, second_filters, rows, cols), "chan"
    )
    x_all = chan_gather(x_pad, "chan")
    x_cols = im2col(x_all)
    pre_full = conv_fwd(x_cols, first_filters, rows, cols)
    pre = pre_full.astype(jnp.bfloat16)
    hidden = jax.nn.silu(pre_full).astype(jnp.bfloat16)
    pre_val = pre.astype(jnp.float32)
    sig = jax.nn.sigmoid(pre_val)
    pre_grad = (hidden_grad * sig * (1.0 + pre_val * (1.0 - sig))).astype(jnp.bfloat16)
    both_pad = extended(jnp.concatenate([hidden, pre_grad]), (("strip", 1),), 1)
    h_pad, da_pad = both_pad[:blocks], both_pad[blocks:]
    h_all = chan_gather(h_pad, "chan")
    h_cols = im2col(h_all)
    (second_grad,) = strip_allreduce((filter_grad(out_grad, h_cols),), "strip")
    output = (features.astype(jnp.float32) + conv_fwd(h_cols, second_filters, rows, cols)).astype(jnp.bfloat16)
    (first_grad,) = strip_allreduce((filter_grad(pre_grad, x_cols),), "strip")
    da_stack = back_stack(da_pad)
    input_term = chan_sum_scatter(
        conv_back_stacked(da_stack, first_filters, rows, cols), "chan"
    )
    input_grad = (out_grad.astype(jnp.float32) + input_term).astype(jnp.bfloat16)
    return (output, input_grad, first_grad, second_grad)


def solution(mesh):
    in_specs = (
        P("chan", "strip", None),
        P("chan", None, None, None),
        P("chan", None, None, None),
        P("chan", "strip", None),
    )
    out_specs = (
        P("chan", "strip", None),
        P("chan", "strip", None),
        P("chan", None, None, None),
        P("chan", None, None, None),
    )
    return jax.shard_map(body, mesh=mesh, in_specs=in_specs, out_specs=out_specs, check_vma=False)
```

```python
import jax
import jax.numpy as jnp
from jax import lax
from jax.sharding import PartitionSpec as P


def extended(cells, sides, width):
    for axis, dim in sides:
        count = lax.axis_size(axis)
        ends = count - 1
        head = lax.slice_in_dim(cells, 0, width, axis=dim)
        tail = lax.slice_in_dim(cells, cells.shape[dim] - width, cells.shape[dim], axis=dim)
        cells = jnp.concatenate(
            [
                lax.ppermute(tail, axis, [(i, (i + 1) % count) for i in range(ends)]),
                cells,
                lax.ppermute(head, axis, [((i + 1) % count, i) for i in range(ends)]),
            ],
            axis=dim,
        )
    return cells


def take_cols(field, shift):
    if shift == 0:
        return field
    edge = jnp.zeros(field.shape[:-1] + (1,), field.dtype)
    if shift > 0:
        return jnp.concatenate([field[..., 1:], edge], axis=-1)
    return jnp.concatenate([edge, field[..., :-1]], axis=-1)


def im2col(padded):
    chans, rows_pad, cols = padded.shape
    rows = rows_pad - 2
    pieces = []
    for kh in range(3):
        for kw in range(3):
            pieces.append(take_cols(padded[:, kh : kh + rows, :], kw - 1))
    return jnp.stack(pieces, axis=0).reshape(9 * chans, rows * cols)


def conv_fwd(cols_in, weight, rows, cols):
    outs = weight.shape[0]
    flat_w = weight.reshape(outs, -1)
    total = jnp.dot(flat_w, cols_in, preferred_element_type=jnp.float32)
    return total.reshape(outs, rows, cols)


def back_stack(padded):
    outs, rows_pad, cols = padded.shape
    rows = rows_pad - 2
    pieces = []
    for kh in range(3):
        for kw in range(3):
            pieces.append(take_cols(padded[:, 2 - kh : 2 - kh + rows, :], 1 - kw))
    return jnp.stack(pieces, axis=1).reshape(outs * 9, rows * cols)


def conv_back_stacked(stacked, weight, rows, cols):
    outs = weight.shape[0]
    inner = weight.shape[3]
    flat_w = weight.reshape(outs * 9, inner)
    result = lax.dot_general(
        flat_w, stacked, (((0,), (0,)), ((), ())), preferred_element_type=jnp.float32
    )
    return result.reshape(inner, rows, cols)


def filter_grad(grad_out, cols_in):
    outs, rows, cols = grad_out.shape
    result = lax.dot_general(
        grad_out.reshape(outs, rows * cols),
        cols_in,
        (((1,), (1,)), ((), ())),
        preferred_element_type=jnp.float32,
    )
    return result.reshape(outs, 3, 3, cols_in.shape[0] // 9)


def chan_sum_scatter(part, axis):
    count = lax.axis_size(axis)
    me = lax.axis_index(axis)
    blocks = part.reshape((count, part.shape[0] // count) + part.shape[1:])
    bit = 1
    while bit < count:
        pairs = blocks.reshape((blocks.shape[0] // 2, 2) + blocks.shape[1:])
        side = (me // bit) % 2
        keep = lax.dynamic_index_in_dim(pairs, side, axis=1, keepdims=False)
        send = lax.dynamic_index_in_dim(pairs, 1 - side, axis=1, keepdims=False)
        blocks = keep + lax.ppermute(send, axis, [(i, i ^ bit) for i in range(count)])
        bit *= 2
    return blocks.reshape(blocks.shape[1:])


def halving_sum(flat, axis, bits):
    me = lax.axis_index(axis)
    count = lax.axis_size(axis)
    for bit in bits:
        pairs = flat.reshape((2, flat.shape[0] // 2) + flat.shape[1:])
        side = (me >> bit) & 1
        keep = lax.dynamic_index_in_dim(pairs, side, axis=0, keepdims=False)
        send = lax.dynamic_index_in_dim(pairs, 1 - side, axis=0, keepdims=False)
        flat = keep + lax.ppermute(send, axis, [(i, i ^ (1 << bit)) for i in range(count)])
    return flat


def halving_gather(part, axis, bits):
    me = lax.axis_index(axis)
    count = lax.axis_size(axis)
    for bit in reversed(bits):
        got = lax.ppermute(part, axis, [(i, i ^ (1 << bit)) for i in range(count)])
        side = (me >> bit) & 1
        part = jnp.where(side == 0, jnp.concatenate([part, got]), jnp.concatenate([got, part]))
    return part


def chan_gather(block, axis):
    levels = lax.axis_size(axis).bit_length() - 1
    return halving_gather(block, axis, tuple(reversed(range(levels))))


def strip_allreduce(terms, axis):
    count = lax.axis_size(axis)
    levels = count.bit_length() - 1
    assert 1 << levels == count
    flat = jnp.concatenate([t.reshape(-1, 128) for t in terms])
    half = flat.shape[0] // 2
    orders = (tuple(range(levels)), (1, 0) + tuple(range(2, levels)))
    outs = []
    for part, bits in zip((flat[:half], flat[half:]), orders):
        summed = halving_sum(part, axis, bits).astype(jnp.bfloat16)
        outs.append(halving_gather(summed, axis, bits))
    flat = jnp.concatenate(outs).astype(jnp.float32)
    results, at = [], 0
    for t in terms:
        results.append(flat[at : at + t.size // 128].reshape(t.shape))
        at += t.size // 128
    return results


def body(features, first_filters, second_filters, out_grad):
    blocks, rows, cols = features.shape
    both_pad = extended(jnp.concatenate([features, out_grad]), (("strip", 1),), 1)
    x_pad, dy_pad = both_pad[:blocks], both_pad[blocks:]
    dy_stack = back_stack(dy_pad)
    hidden_grad = chan_sum_scatter(
        conv_back_stacked(dy_stack, second_filters, rows, cols), "chan"
    )
    x_all = chan_gather(x_pad, "chan")
    x_cols = im2col(x_all)
    pre_full = conv_fwd(x_cols, first_filters, rows, cols)
    pre = pre_full.astype(jnp.bfloat16)
    hidden = jax.nn.silu(pre_full).astype(jnp.bfloat16)
    pre_val = pre.astype(jnp.float32)
    sig = jax.nn.sigmoid(pre_val)
    pre_grad = (hidden_grad * sig * (1.0 + pre_val * (1.0 - sig))).astype(jnp.bfloat16)
    both_pad = extended(jnp.concatenate([hidden, pre_grad]), (("strip", 1),), 1)
    h_pad, da_pad = both_pad[:blocks], both_pad[blocks:]
    h_all = chan_gather(h_pad, "chan")
    h_cols = im2col(h_all)
    (second_grad,) = strip_allreduce((filter_grad(out_grad, h_cols),), "strip")
    output = (features.astype(jnp.float32) + conv_fwd(h_cols, second_filters, rows, cols)).astype(jnp.bfloat16)
    (first_grad,) = strip_allreduce((filter_grad(pre_grad, x_cols),), "strip")
    da_stack = back_stack(da_pad)
    input_term = chan_sum_scatter(
        conv_back_stacked(da_stack, first_filters, rows, cols), "chan"
    )
    input_grad = (out_grad.astype(jnp.float32) + input_term).astype(jnp.bfloat16)
    return (output, input_grad, first_grad, second_grad)


def solution(mesh):
    in_specs = (
        P("chan", "strip", None),
        P("chan", None, None, None),
        P("chan", None, None, None),
        P("chan", "strip", None),
    )
    out_specs = (
        P("chan", "strip", None),
        P("chan", "strip", None),
        P("chan", None, None, None),
        P("chan", None, None, None),
    )
    return jax.shard_map(body, mesh=mesh, in_specs=in_specs, out_specs=out_specs, check_vma=False)
```

```python
import jax
import jax.numpy as jnp
from jax import lax
from jax.sharding import PartitionSpec as P


def extended(cells, sides, width):
    for axis, dim in sides:
        count = lax.axis_size(axis)
        ends = count - 1
        head = lax.slice_in_dim(cells, 0, width, axis=dim)
        tail = lax.slice_in_dim(cells, cells.shape[dim] - width, cells.shape[dim], axis=dim)
        cells = jnp.concatenate(
            [
                lax.ppermute(tail, axis, [(i, (i + 1) % count) for i in range(ends)]),
                cells,
                lax.ppermute(head, axis, [((i + 1) % count, i) for i in range(ends)]),
            ],
            axis=dim,
        )
    return cells


def take_cols(field, shift):
    if shift == 0:
        return field
    edge = jnp.zeros(field.shape[:-1] + (1,), field.dtype)
    if shift > 0:
        return jnp.concatenate([field[..., 1:], edge], axis=-1)
    return jnp.concatenate([edge, field[..., :-1]], axis=-1)


def im2col(padded):
    chans, rows_pad, cols = padded.shape
    rows = rows_pad - 2
    pieces = []
    for kh in range(3):
        for kw in range(3):
            pieces.append(take_cols(padded[:, kh : kh + rows, :], kw - 1))
    return jnp.stack(pieces, axis=0).reshape(9 * chans, rows * cols)


def conv_fwd(cols_in, weight, rows, cols):
    outs = weight.shape[0]
    flat_w = weight.reshape(outs, -1)
    total = jnp.dot(flat_w, cols_in, preferred_element_type=jnp.float32)
    return total.reshape(outs, rows, cols)


def back_stack(padded):
    outs, rows_pad, cols = padded.shape
    rows = rows_pad - 2
    pieces = []
    for kh in range(3):
        for kw in range(3):
            pieces.append(take_cols(padded[:, 2 - kh : 2 - kh + rows, :], 1 - kw))
    return jnp.stack(pieces, axis=1).reshape(outs * 9, rows * cols)


def conv_back_stacked(stacked, weight, rows, cols):
    outs = weight.shape[0]
    inner = weight.shape[3]
    flat_w = weight.reshape(outs * 9, inner)
    result = lax.dot_general(
        flat_w, stacked, (((0,), (0,)), ((), ())), preferred_element_type=jnp.float32
    )
    return result.reshape(inner, rows, cols)


def filter_grad(grad_out, cols_in):
    outs, rows, cols = grad_out.shape
    result = lax.dot_general(
        grad_out.reshape(outs, rows * cols),
        cols_in,
        (((1,), (1,)), ((), ())),
        preferred_element_type=jnp.float32,
    )
    return result.reshape(outs, 3, 3, cols_in.shape[0] // 9)


def chan_sum_scatter(part, axis):
    count = lax.axis_size(axis)
    me = lax.axis_index(axis)
    blocks = part.reshape((count, part.shape[0] // count) + part.shape[1:])
    bit = 1
    while bit < count:
        pairs = blocks.reshape((blocks.shape[0] // 2, 2) + blocks.shape[1:])
        side = (me // bit) % 2
        keep = lax.dynamic_index_in_dim(pairs, side, axis=1, keepdims=False)
        send = lax.dynamic_index_in_dim(pairs, 1 - side, axis=1, keepdims=False)
        blocks = keep + lax.ppermute(send, axis, [(i, i ^ bit) for i in range(count)])
        bit *= 2
    return blocks.reshape(blocks.shape[1:])


def halving_sum(flat, axis, bits):
    me = lax.axis_index(axis)
    count = lax.axis_size(axis)
    for bit in bits:
        pairs = flat.reshape((2, flat.shape[0] // 2) + flat.shape[1:])
        side = (me >> bit) & 1
        keep = lax.dynamic_index_in_dim(pairs, side, axis=0, keepdims=False)
        send = lax.dynamic_index_in_dim(pairs, 1 - side, axis=0, keepdims=False)
        flat = keep + lax.ppermute(send, axis, [(i, i ^ (1 << bit)) for i in range(count)])
    return flat


def halving_gather(part, axis, bits):
    me = lax.axis_index(axis)
    count = lax.axis_size(axis)
    for bit in reversed(bits):
        got = lax.ppermute(part, axis, [(i, i ^ (1 << bit)) for i in range(count)])
        side = (me >> bit) & 1
        part = jnp.where(side == 0, jnp.concatenate([part, got]), jnp.concatenate([got, part]))
    return part


def chan_gather(block, axis):
    levels = lax.axis_size(axis).bit_length() - 1
    return halving_gather(block, axis, tuple(reversed(range(levels))))


def strip_allreduce(terms, axis):
    count = lax.axis_size(axis)
    levels = count.bit_length() - 1
    assert 1 << levels == count
    flat = jnp.concatenate([t.reshape(-1, 128) for t in terms])
    half = flat.shape[0] // 2
    orders = (tuple(range(levels)), (1, 0) + tuple(range(2, levels)))
    outs = []
    for part, bits in zip((flat[:half], flat[half:]), orders):
        summed = halving_sum(part, axis, bits).astype(jnp.bfloat16)
        outs.append(halving_gather(summed, axis, bits))
    flat = jnp.concatenate(outs).astype(jnp.float32)
    results, at = [], 0
    for t in terms:
        results.append(flat[at : at + t.size // 128].reshape(t.shape))
        at += t.size // 128
    return results


def body(features, first_filters, second_filters, out_grad):
    blocks, rows, cols = features.shape
    both_pad = extended(jnp.concatenate([features, out_grad]), (("strip", 1),), 1)
    x_pad, dy_pad = both_pad[:blocks], both_pad[blocks:]
    dy_stack = back_stack(dy_pad)
    hidden_grad = chan_sum_scatter(
        conv_back_stacked(dy_stack, second_filters, 1, rows * cols).reshape(-1, rows * cols), "chan"
    ).reshape(-1, rows, cols)
    x_all = chan_gather(x_pad, "chan")
    x_cols = im2col(x_all)
    pre_full = conv_fwd(x_cols, first_filters, rows, cols)
    pre = pre_full.astype(jnp.bfloat16)
    hidden = jax.nn.silu(pre_full).astype(jnp.bfloat16)
    pre_val = pre.astype(jnp.float32)
    sig = jax.nn.sigmoid(pre_val)
    pre_grad = (hidden_grad * sig * (1.0 + pre_val * (1.0 - sig))).astype(jnp.bfloat16)
    both_pad = extended(jnp.concatenate([hidden, pre_grad]), (("strip", 1),), 1)
    h_pad, da_pad = both_pad[:blocks], both_pad[blocks:]
    h_all = chan_gather(h_pad, "chan")
    h_cols = im2col(h_all)
    (second_grad,) = strip_allreduce((filter_grad(out_grad, h_cols),), "strip")
    output = (features.astype(jnp.float32) + conv_fwd(h_cols, second_filters, rows, cols)).astype(jnp.bfloat16)
    (first_grad,) = strip_allreduce((filter_grad(pre_grad, x_cols),), "strip")
    da_stack = back_stack(da_pad)
    input_term = chan_sum_scatter(
        conv_back_stacked(da_stack, first_filters, 1, rows * cols).reshape(-1, rows * cols), "chan"
    ).reshape(-1, rows, cols)
    input_grad = (out_grad.astype(jnp.float32) + input_term).astype(jnp.bfloat16)
    return (output, input_grad, first_grad, second_grad)


def solution(mesh):
    in_specs = (
        P("chan", "strip", None),
        P("chan", None, None, None),
        P("chan", None, None, None),
        P("chan", "strip", None),
    )
    out_specs = (
        P("chan", "strip", None),
        P("chan", "strip", None),
        P("chan", None, None, None),
        P("chan", None, None, None),
    )
    return jax.shard_map(body, mesh=mesh, in_specs=in_specs, out_specs=out_specs, check_vma=False)
```

```python
import jax
import jax.numpy as jnp
from jax import lax
from jax.sharding import PartitionSpec as P


def extended(cells, sides, width):
    for axis, dim in sides:
        count = lax.axis_size(axis)
        ends = count - 1
        head = lax.slice_in_dim(cells, 0, width, axis=dim)
        tail = lax.slice_in_dim(cells, cells.shape[dim] - width, cells.shape[dim], axis=dim)
        flat = width == 1
        if flat:
            head, tail = jnp.squeeze(head, dim), jnp.squeeze(tail, dim)
        before = lax.ppermute(tail, axis, [(i, (i + 1) % count) for i in range(ends)])
        after = lax.ppermute(head, axis, [((i + 1) % count, i) for i in range(ends)])
        if flat:
            before, after = jnp.expand_dims(before, dim), jnp.expand_dims(after, dim)
        cells = jnp.concatenate([before, cells, after], axis=dim)
    return cells


def take_cols(field, shift):
    if shift == 0:
        return field
    edge = jnp.zeros(field.shape[:-1] + (1,), field.dtype)
    if shift > 0:
        return jnp.concatenate([field[..., 1:], edge], axis=-1)
    return jnp.concatenate([edge, field[..., :-1]], axis=-1)


def im2col(padded):
    chans, rows_pad, cols = padded.shape
    rows = rows_pad - 2
    pieces = []
    for kh in range(3):
        for kw in range(3):
            pieces.append(take_cols(padded[:, kh : kh + rows, :], kw - 1))
    return jnp.stack(pieces, axis=0).reshape(9 * chans, rows * cols)


def conv_fwd(cols_in, weight, rows, cols):
    outs = weight.shape[0]
    flat_w = weight.reshape(outs, -1)
    total = jnp.dot(flat_w, cols_in, preferred_element_type=jnp.float32)
    return total.reshape(outs, rows, cols)


def back_stack(padded):
    outs, rows_pad, cols = padded.shape
    rows = rows_pad - 2
    pieces = []
    for kh in range(3):
        for kw in range(3):
            pieces.append(take_cols(padded[:, 2 - kh : 2 - kh + rows, :], 1 - kw))
    return jnp.stack(pieces, axis=1).reshape(outs * 9, rows * cols)


def conv_back_stacked(stacked, weight, rows, cols):
    outs = weight.shape[0]
    inner = weight.shape[3]
    flat_w = weight.reshape(outs * 9, inner)
    result = lax.dot_general(
        flat_w, stacked, (((0,), (0,)), ((), ())), preferred_element_type=jnp.float32
    )
    return result.reshape(inner, rows, cols)


def filter_grad(grad_out, cols_in):
    outs, rows, cols = grad_out.shape
    result = lax.dot_general(
        grad_out.reshape(outs, rows * cols),
        cols_in,
        (((1,), (1,)), ((), ())),
        preferred_element_type=jnp.float32,
    )
    return result.reshape(outs, 3, 3, cols_in.shape[0] // 9)


def chan_sum_scatter(part, axis):
    count = lax.axis_size(axis)
    me = lax.axis_index(axis)
    blocks = part.reshape((count, part.shape[0] // count) + part.shape[1:])
    bit = 1
    while bit < count:
        pairs = blocks.reshape((blocks.shape[0] // 2, 2) + blocks.shape[1:])
        side = (me // bit) % 2
        keep = lax.dynamic_index_in_dim(pairs, side, axis=1, keepdims=False)
        send = lax.dynamic_index_in_dim(pairs, 1 - side, axis=1, keepdims=False)
        blocks = keep + lax.ppermute(send, axis, [(i, i ^ bit) for i in range(count)])
        bit *= 2
    return blocks.reshape(blocks.shape[1:])


def halving_sum(flat, axis, bits):
    me = lax.axis_index(axis)
    count = lax.axis_size(axis)
    for bit in bits:
        pairs = flat.reshape((2, flat.shape[0] // 2) + flat.shape[1:])
        side = (me >> bit) & 1
        keep = lax.dynamic_index_in_dim(pairs, side, axis=0, keepdims=False)
        send = lax.dynamic_index_in_dim(pairs, 1 - side, axis=0, keepdims=False)
        flat = keep + lax.ppermute(send, axis, [(i, i ^ (1 << bit)) for i in range(count)])
    return flat


def halving_gather(part, axis, bits):
    me = lax.axis_index(axis)
    count = lax.axis_size(axis)
    for bit in reversed(bits):
        got = lax.ppermute(part, axis, [(i, i ^ (1 << bit)) for i in range(count)])
        side = (me >> bit) & 1
        part = jnp.where(side == 0, jnp.concatenate([part, got]), jnp.concatenate([got, part]))
    return part


def chan_gather(block, axis):
    levels = lax.axis_size(axis).bit_length() - 1
    return halving_gather(block, axis, tuple(reversed(range(levels))))


def strip_allreduce(terms, axis):
    count = lax.axis_size(axis)
    levels = count.bit_length() - 1
    assert 1 << levels == count
    flat = jnp.concatenate([t.reshape(-1, 128) for t in terms])
    half = flat.shape[0] // 2
    orders = (tuple(range(levels)), (1, 0) + tuple(range(2, levels)))
    outs = []
    for part, bits in zip((flat[:half], flat[half:]), orders):
        summed = halving_sum(part, axis, bits).astype(jnp.bfloat16)
        outs.append(halving_gather(summed, axis, bits))
    flat = jnp.concatenate(outs).astype(jnp.float32)
    results, at = [], 0
    for t in terms:
        results.append(flat[at : at + t.size // 128].reshape(t.shape))
        at += t.size // 128
    return results


def body(features, first_filters, second_filters, out_grad):
    blocks, rows, cols = features.shape
    both_pad = extended(jnp.concatenate([features, out_grad]), (("strip", 1),), 1)
    x_pad, dy_pad = both_pad[:blocks], both_pad[blocks:]
    dy_stack = back_stack(dy_pad)
    hidden_grad = chan_sum_scatter(
        conv_back_stacked(dy_stack, second_filters, 1, rows * cols).reshape(-1, rows * cols), "chan"
    ).reshape(-1, rows, cols)
    x_all = chan_gather(x_pad, "chan")
    x_cols = im2col(x_all)
    pre_full = conv_fwd(x_cols, first_filters, rows, cols)
    pre = pre_full.astype(jnp.bfloat16)
    hidden = jax.nn.silu(pre_full).astype(jnp.bfloat16)
    pre_val = pre.astype(jnp.float32)
    sig = jax.nn.sigmoid(pre_val)
    pre_grad = (hidden_grad * sig * (1.0 + pre_val * (1.0 - sig))).astype(jnp.bfloat16)
    both_pad = extended(jnp.concatenate([hidden, pre_grad]), (("strip", 1),), 1)
    h_pad, da_pad = both_pad[:blocks], both_pad[blocks:]
    h_all = chan_gather(h_pad, "chan")
    h_cols = im2col(h_all)
    (second_grad,) = strip_allreduce((filter_grad(out_grad, h_cols),), "strip")
    output = (features.astype(jnp.float32) + conv_fwd(h_cols, second_filters, rows, cols)).astype(jnp.bfloat16)
    (first_grad,) = strip_allreduce((filter_grad(pre_grad, x_cols),), "strip")
    da_stack = back_stack(da_pad)
    input_term = chan_sum_scatter(
        conv_back_stacked(da_stack, first_filters, 1, rows * cols).reshape(-1, rows * cols), "chan"
    ).reshape(-1, rows, cols)
    input_grad = (out_grad.astype(jnp.float32) + input_term).astype(jnp.bfloat16)
    return (output, input_grad, first_grad, second_grad)


def solution(mesh):
    in_specs = (
        P("chan", "strip", None),
        P("chan", None, None, None),
        P("chan", None, None, None),
        P("chan", "strip", None),
    )
    out_specs = (
        P("chan", "strip", None),
        P("chan", "strip", None),
        P("chan", None, None, None),
        P("chan", None, None, None),
    )
    return jax.shard_map(body, mesh=mesh, in_specs=in_specs, out_specs=out_specs, check_vma=False)
```

```python
import jax
import jax.numpy as jnp
from jax import lax
from jax.sharding import PartitionSpec as P


def extended(cells, sides, width):
    for axis, dim in sides:
        count = lax.axis_size(axis)
        ends = count - 1
        head = lax.slice_in_dim(cells, 0, width, axis=dim)
        tail = lax.slice_in_dim(cells, cells.shape[dim] - width, cells.shape[dim], axis=dim)
        cells = jnp.concatenate(
            [
                lax.ppermute(tail, axis, [(i, (i + 1) % count) for i in range(ends)]),
                cells,
                lax.ppermute(head, axis, [((i + 1) % count, i) for i in range(ends)]),
            ],
            axis=dim,
        )
    return cells


def take_cols(field, shift):
    if shift == 0:
        return field
    edge = jnp.zeros(field.shape[:-1] + (1,), field.dtype)
    if shift > 0:
        return jnp.concatenate([field[..., 1:], edge], axis=-1)
    return jnp.concatenate([edge, field[..., :-1]], axis=-1)


def im2col(padded):
    chans, rows_pad, cols = padded.shape
    rows = rows_pad - 2
    pieces = []
    for kh in range(3):
        for kw in range(3):
            pieces.append(take_cols(padded[:, kh : kh + rows, :], kw - 1))
    return jnp.stack(pieces, axis=0).reshape(9 * chans, rows * cols)


def conv_fwd(cols_in, weight, rows, cols):
    outs = weight.shape[0]
    flat_w = weight.reshape(outs, -1)
    total = jnp.dot(flat_w, cols_in, preferred_element_type=jnp.float32)
    return total.reshape(outs, rows, cols)


def back_stack(padded):
    outs, rows_pad, cols = padded.shape
    rows = rows_pad - 2
    pieces = []
    for kh in range(3):
        for kw in range(3):
            pieces.append(take_cols(padded[:, 2 - kh : 2 - kh + rows, :], 1 - kw))
    return jnp.stack(pieces, axis=1).reshape(outs * 9, rows * cols)


def conv_back_stacked(stacked, weight, rows, cols):
    outs = weight.shape[0]
    inner = weight.shape[3]
    flat_w = weight.reshape(outs * 9, inner)
    result = lax.dot_general(
        flat_w, stacked, (((0,), (0,)), ((), ())), preferred_element_type=jnp.float32
    )
    return result.reshape(inner, rows, cols)


def filter_grad(grad_out, cols_in):
    outs, rows, cols = grad_out.shape
    result = lax.dot_general(
        grad_out.reshape(outs, rows * cols),
        cols_in,
        (((1,), (1,)), ((), ())),
        preferred_element_type=jnp.float32,
    )
    return result.reshape(outs, 3, 3, cols_in.shape[0] // 9)


def chan_sum_scatter(part, axis):
    count = lax.axis_size(axis)
    me = lax.axis_index(axis)
    blocks = part.reshape((count, part.shape[0] // count) + part.shape[1:])
    bit = 1
    while bit < count:
        pairs = blocks.reshape((blocks.shape[0] // 2, 2) + blocks.shape[1:])
        side = (me // bit) % 2
        keep = lax.dynamic_index_in_dim(pairs, side, axis=1, keepdims=False)
        send = lax.dynamic_index_in_dim(pairs, 1 - side, axis=1, keepdims=False)
        blocks = keep + lax.ppermute(send, axis, [(i, i ^ bit) for i in range(count)])
        bit *= 2
    return blocks.reshape(blocks.shape[1:])


def halving_sum(flat, axis, bits):
    me = lax.axis_index(axis)
    count = lax.axis_size(axis)
    for bit in bits:
        pairs = flat.reshape((2, flat.shape[0] // 2) + flat.shape[1:])
        side = (me >> bit) & 1
        keep = lax.dynamic_index_in_dim(pairs, side, axis=0, keepdims=False)
        send = lax.dynamic_index_in_dim(pairs, 1 - side, axis=0, keepdims=False)
        flat = keep + lax.ppermute(send, axis, [(i, i ^ (1 << bit)) for i in range(count)])
    return flat


def halving_gather(part, axis, bits):
    me = lax.axis_index(axis)
    count = lax.axis_size(axis)
    for bit in reversed(bits):
        got = lax.ppermute(part, axis, [(i, i ^ (1 << bit)) for i in range(count)])
        side = (me >> bit) & 1
        part = jnp.where(side == 0, jnp.concatenate([part, got]), jnp.concatenate([got, part]))
    return part


def chan_gather(block, axis):
    levels = lax.axis_size(axis).bit_length() - 1
    return halving_gather(block, axis, tuple(reversed(range(levels))))


def strip_allreduce(terms, axis):
    count = lax.axis_size(axis)
    levels = count.bit_length() - 1
    assert 1 << levels == count
    flat = jnp.concatenate([t.reshape(-1, 128) for t in terms])
    half = flat.shape[0] // 2
    orders = (tuple(range(levels)), (1, 0) + tuple(range(2, levels)))
    outs = []
    for part, bits in zip((flat[:half], flat[half:]), orders):
        summed = halving_sum(part, axis, bits).astype(jnp.bfloat16)
        outs.append(halving_gather(summed, axis, bits))
    flat = jnp.concatenate(outs).astype(jnp.float32)
    results, at = [], 0
    for t in terms:
        results.append(flat[at : at + t.size // 128].reshape(t.shape))
        at += t.size // 128
    return results


def body(features, first_filters, second_filters, out_grad):
    blocks, rows, cols = features.shape
    both_pad = extended(jnp.concatenate([features, out_grad]), (("strip", 1),), 1)
    x_pad, dy_pad = both_pad[:blocks], both_pad[blocks:]
    dy_stack = back_stack(dy_pad)
    hidden_grad = chan_sum_scatter(
        conv_back_stacked(dy_stack, second_filters, 1, rows * cols).reshape(-1, rows * cols), "chan"
    ).reshape(-1, rows, cols)
    x_all = chan_gather(x_pad.reshape(blocks, -1), "chan").reshape(-1, rows + 2, cols)
    x_cols = im2col(x_all)
    pre_full = conv_fwd(x_cols, first_filters, rows, cols)
    pre = pre_full.astype(jnp.bfloat16)
    hidden = jax.nn.silu(pre_full).astype(jnp.bfloat16)
    pre_val = pre.astype(jnp.float32)
    sig = jax.nn.sigmoid(pre_val)
    pre_grad = (hidden_grad * sig * (1.0 + pre_val * (1.0 - sig))).astype(jnp.bfloat16)
    both_pad = extended(jnp.concatenate([hidden, pre_grad]), (("strip", 1),), 1)
    h_pad, da_pad = both_pad[:blocks], both_pad[blocks:]
    h_all = chan_gather(h_pad.reshape(blocks, -1), "chan").reshape(-1, rows + 2, cols)
    h_cols = im2col(h_all)
    (second_grad,) = strip_allreduce((filter_grad(out_grad, h_cols),), "strip")
    output = (features.astype(jnp.float32) + conv_fwd(h_cols, second_filters, rows, cols)).astype(jnp.bfloat16)
    (first_grad,) = strip_allreduce((filter_grad(pre_grad, x_cols),), "strip")
    da_stack = back_stack(da_pad)
    input_term = chan_sum_scatter(
        conv_back_stacked(da_stack, first_filters, 1, rows * cols).reshape(-1, rows * cols), "chan"
    ).reshape(-1, rows, cols)
    input_grad = (out_grad.astype(jnp.float32) + input_term).astype(jnp.bfloat16)
    return (output, input_grad, first_grad, second_grad)


def solution(mesh):
    in_specs = (
        P("chan", "strip", None),
        P("chan", None, None, None),
        P("chan", None, None, None),
        P("chan", "strip", None),
    )
    out_specs = (
        P("chan", "strip", None),
        P("chan", "strip", None),
        P("chan", None, None, None),
        P("chan", None, None, None),
    )
    return jax.shard_map(body, mesh=mesh, in_specs=in_specs, out_specs=out_specs, check_vma=False)
```

```python
import jax
import jax.numpy as jnp
from jax import lax
from jax.sharding import PartitionSpec as P


def extended(cells, sides, width):
    for axis, dim in sides:
        count = lax.axis_size(axis)
        ends = count - 1
        head = lax.slice_in_dim(cells, 0, width, axis=dim)
        tail = lax.slice_in_dim(cells, cells.shape[dim] - width, cells.shape[dim], axis=dim)
        cells = jnp.concatenate(
            [
                lax.ppermute(tail, axis, [(i, (i + 1) % count) for i in range(ends)]),
                cells,
                lax.ppermute(head, axis, [((i + 1) % count, i) for i in range(ends)]),
            ],
            axis=dim,
        )
    return cells


def take_cols(field, shift):
    if shift == 0:
        return field
    edge = jnp.zeros(field.shape[:-1] + (1,), field.dtype)
    if shift > 0:
        return jnp.concatenate([field[..., 1:], edge], axis=-1)
    return jnp.concatenate([edge, field[..., :-1]], axis=-1)


def im2col(padded):
    chans, rows_pad, cols = padded.shape
    rows = rows_pad - 2
    pieces = []
    for kh in range(3):
        for kw in range(3):
            pieces.append(take_cols(padded[:, kh : kh + rows, :], kw - 1))
    return jnp.stack(pieces, axis=0).reshape(9 * chans, rows * cols)


def conv_fwd(cols_in, weight, rows, cols):
    outs = weight.shape[0]
    flat_w = weight.reshape(outs, -1)
    total = jnp.dot(flat_w, cols_in, preferred_element_type=jnp.float32)
    return total.reshape(outs, rows, cols)


def back_stack(padded):
    outs, rows_pad, cols = padded.shape
    rows = rows_pad - 2
    pieces = []
    for kh in range(3):
        for kw in range(3):
            pieces.append(take_cols(padded[:, 2 - kh : 2 - kh + rows, :], 1 - kw))
    return jnp.stack(pieces, axis=1).reshape(outs * 9, rows * cols)


def conv_back_stacked(stacked, weight, rows, cols):
    outs = weight.shape[0]
    inner = weight.shape[3]
    flat_w = weight.reshape(outs * 9, inner)
    result = lax.dot_general(
        flat_w, stacked, (((0,), (0,)), ((), ())), preferred_element_type=jnp.float32
    )
    return result.reshape(inner, rows, cols)


def filter_grad(grad_out, cols_in):
    outs, rows, cols = grad_out.shape
    result = lax.dot_general(
        grad_out.reshape(outs, rows * cols),
        cols_in,
        (((1,), (1,)), ((), ())),
        preferred_element_type=jnp.float32,
    )
    return result.reshape(outs, 3, 3, cols_in.shape[0] // 9)


def chan_sum_scatter(part, axis):
    count = lax.axis_size(axis)
    me = lax.axis_index(axis)
    blocks = part.reshape((count, part.shape[0] // count) + part.shape[1:])
    bit = 1
    while bit < count:
        pairs = blocks.reshape((blocks.shape[0] // 2, 2) + blocks.shape[1:])
        side = (me // bit) % 2
        keep = lax.dynamic_index_in_dim(pairs, side, axis=1, keepdims=False)
        send = lax.dynamic_index_in_dim(pairs, 1 - side, axis=1, keepdims=False)
        blocks = keep + lax.ppermute(send, axis, [(i, i ^ bit) for i in range(count)])
        bit *= 2
    return blocks.reshape(blocks.shape[1:])


def halving_sum(flat, axis, bits):
    me = lax.axis_index(axis)
    count = lax.axis_size(axis)
    for bit in bits:
        pairs = flat.reshape((2, flat.shape[0] // 2) + flat.shape[1:])
        side = (me >> bit) & 1
        keep = lax.dynamic_index_in_dim(pairs, side, axis=0, keepdims=False)
        send = lax.dynamic_index_in_dim(pairs, 1 - side, axis=0, keepdims=False)
        flat = keep + lax.ppermute(send, axis, [(i, i ^ (1 << bit)) for i in range(count)])
    return flat


def halving_gather(part, axis, bits):
    me = lax.axis_index(axis)
    count = lax.axis_size(axis)
    for bit in reversed(bits):
        got = lax.ppermute(part, axis, [(i, i ^ (1 << bit)) for i in range(count)])
        side = (me >> bit) & 1
        part = jnp.where(side == 0, jnp.concatenate([part, got]), jnp.concatenate([got, part]))
    return part


def chan_gather(block, axis):
    levels = lax.axis_size(axis).bit_length() - 1
    return halving_gather(block, axis, tuple(reversed(range(levels))))


def strip_allreduce(terms, axis):
    count = lax.axis_size(axis)
    levels = count.bit_length() - 1
    assert 1 << levels == count
    total = sum(t.size for t in terms)
    lane = 512 if total % (512 * 16 * count) == 0 else 128
    flat = jnp.concatenate([t.reshape(-1, lane) for t in terms])
    half = flat.shape[0] // 2
    orders = (tuple(range(levels)), (1, 0) + tuple(range(2, levels)))
    outs = []
    for part, bits in zip((flat[:half], flat[half:]), orders):
        summed = halving_sum(part, axis, bits).astype(jnp.bfloat16)
        outs.append(halving_gather(summed, axis, bits))
    flat = jnp.concatenate(outs).astype(jnp.float32)
    results, at = [], 0
    for t in terms:
        results.append(flat[at : at + t.size // lane].reshape(t.shape))
        at += t.size // lane
    return results


def body(features, first_filters, second_filters, out_grad):
    blocks, rows, cols = features.shape
    both_pad = extended(jnp.concatenate([features, out_grad]), (("strip", 1),), 1)
    x_pad, dy_pad = both_pad[:blocks], both_pad[blocks:]
    dy_stack = back_stack(dy_pad)
    hidden_grad = chan_sum_scatter(
        conv_back_stacked(dy_stack, second_filters, 1, rows * cols).reshape(-1, rows * cols), "chan"
    ).reshape(-1, rows, cols)
    x_all = chan_gather(x_pad, "chan")
    x_cols = im2col(x_all)
    pre_full = conv_fwd(x_cols, first_filters, rows, cols)
    pre = pre_full.astype(jnp.bfloat16)
    hidden = jax.nn.silu(pre_full).astype(jnp.bfloat16)
    pre_val = pre.astype(jnp.float32)
    sig = jax.nn.sigmoid(pre_val)
    pre_grad = (hidden_grad * sig * (1.0 + pre_val * (1.0 - sig))).astype(jnp.bfloat16)
    both_pad = extended(jnp.concatenate([hidden, pre_grad]), (("strip", 1),), 1)
    h_pad, da_pad = both_pad[:blocks], both_pad[blocks:]
    h_all = chan_gather(h_pad, "chan")
    h_cols = im2col(h_all)
    (second_grad,) = strip_allreduce((filter_grad(out_grad, h_cols),), "strip")
    output = (features.astype(jnp.float32) + conv_fwd(h_cols, second_filters, rows, cols)).astype(jnp.bfloat16)
    (first_grad,) = strip_allreduce((filter_grad(pre_grad, x_cols),), "strip")
    da_stack = back_stack(da_pad)
    input_term = chan_sum_scatter(
        conv_back_stacked(da_stack, first_filters, 1, rows * cols).reshape(-1, rows * cols), "chan"
    ).reshape(-1, rows, cols)
    input_grad = (out_grad.astype(jnp.float32) + input_term).astype(jnp.bfloat16)
    return (output, input_grad, first_grad, second_grad)


def solution(mesh):
    in_specs = (
        P("chan", "strip", None),
        P("chan", None, None, None),
        P("chan", None, None, None),
        P("chan", "strip", None),
    )
    out_specs = (
        P("chan", "strip", None),
        P("chan", "strip", None),
        P("chan", None, None, None),
        P("chan", None, None, None),
    )
    return jax.shard_map(body, mesh=mesh, in_specs=in_specs, out_specs=out_specs, check_vma=False)
```

```python
import jax
import jax.numpy as jnp
from jax import lax
from jax.sharding import PartitionSpec as P


def extended(cells, sides, width):
    for axis, dim in sides:
        count = lax.axis_size(axis)
        ends = count - 1
        head = lax.slice_in_dim(cells, 0, width, axis=dim)
        tail = lax.slice_in_dim(cells, cells.shape[dim] - width, cells.shape[dim], axis=dim)
        cells = jnp.concatenate(
            [
                lax.ppermute(tail, axis, [(i, (i + 1) % count) for i in range(ends)]),
                cells,
                lax.ppermute(head, axis, [((i + 1) % count, i) for i in range(ends)]),
            ],
            axis=dim,
        )
    return cells


def take_cols(field, shift):
    if shift == 0:
        return field
    edge = jnp.zeros(field.shape[:-1] + (1,), field.dtype)
    if shift > 0:
        return jnp.concatenate([field[..., 1:], edge], axis=-1)
    return jnp.concatenate([edge, field[..., :-1]], axis=-1)


def im2col(padded):
    chans, rows_pad, cols = padded.shape
    rows = rows_pad - 2
    pieces = []
    for kh in range(3):
        for kw in range(3):
            pieces.append(take_cols(padded[:, kh : kh + rows, :], kw - 1))
    return jnp.stack(pieces, axis=0).reshape(9 * chans, rows * cols)


def conv_fwd(cols_in, weight, rows, cols):
    outs = weight.shape[0]
    flat_w = weight.reshape(outs, -1)
    total = jnp.dot(flat_w, cols_in, preferred_element_type=jnp.float32)
    return total.reshape(outs, rows, cols)


def back_stack(padded):
    outs, rows_pad, cols = padded.shape
    rows = rows_pad - 2
    pieces = []
    for kh in range(3):
        for kw in range(3):
            pieces.append(take_cols(padded[:, 2 - kh : 2 - kh + rows, :], 1 - kw))
    return jnp.stack(pieces, axis=1).reshape(outs * 9, rows * cols)


def conv_back_stacked(stacked, weight, rows, cols):
    outs = weight.shape[0]
    inner = weight.shape[3]
    flat_w = weight.reshape(outs * 9, inner)
    result = lax.dot_general(
        flat_w, stacked, (((0,), (0,)), ((), ())), preferred_element_type=jnp.float32
    )
    return result.reshape(inner, rows, cols)


def filter_grad(grad_out, cols_in):
    outs, rows, cols = grad_out.shape
    result = lax.dot_general(
        grad_out.reshape(outs, rows * cols),
        cols_in,
        (((1,), (1,)), ((), ())),
        preferred_element_type=jnp.float32,
    )
    return result.reshape(outs, 3, 3, cols_in.shape[0] // 9)


def chan_sum_scatter(part, axis):
    count = lax.axis_size(axis)
    me = lax.axis_index(axis)
    blocks = part.reshape((count, part.shape[0] // count) + part.shape[1:])
    bit = 1
    while bit < count:
        pairs = blocks.reshape((blocks.shape[0] // 2, 2) + blocks.shape[1:])
        side = (me // bit) % 2
        keep = lax.dynamic_index_in_dim(pairs, side, axis=1, keepdims=False)
        send = lax.dynamic_index_in_dim(pairs, 1 - side, axis=1, keepdims=False)
        blocks = keep + lax.ppermute(send, axis, [(i, i ^ bit) for i in range(count)])
        bit *= 2
    return blocks.reshape(blocks.shape[1:])


def halving_sum(flat, axis, bits):
    me = lax.axis_index(axis)
    count = lax.axis_size(axis)
    for bit in bits:
        pairs = flat.reshape((2, flat.shape[0] // 2) + flat.shape[1:])
        side = (me >> bit) & 1
        keep = lax.dynamic_index_in_dim(pairs, side, axis=0, keepdims=False)
        send = lax.dynamic_index_in_dim(pairs, 1 - side, axis=0, keepdims=False)
        flat = keep + lax.ppermute(send, axis, [(i, i ^ (1 << bit)) for i in range(count)])
    return flat


def halving_gather(part, axis, bits):
    me = lax.axis_index(axis)
    count = lax.axis_size(axis)
    for bit in reversed(bits):
        got = lax.ppermute(part, axis, [(i, i ^ (1 << bit)) for i in range(count)])
        side = (me >> bit) & 1
        part = jnp.where(side == 0, jnp.concatenate([part, got]), jnp.concatenate([got, part]))
    return part


def chan_gather(block, axis):
    levels = lax.axis_size(axis).bit_length() - 1
    return halving_gather(block, axis, tuple(reversed(range(levels))))


def strip_allreduce(terms, axis):
    count = lax.axis_size(axis)
    levels = count.bit_length() - 1
    assert 1 << levels == count
    total = sum(t.size for t in terms)
    widths = (terms[0].size // terms[0].shape[0], 512, 128)
    lane = next(w for w in widths if total % (w * 16 * count) == 0 or w == 128)
    flat = jnp.concatenate([t.reshape(-1, lane) for t in terms])
    half = flat.shape[0] // 2
    orders = (tuple(range(levels)), (1, 0) + tuple(range(2, levels)))
    outs = []
    for part, bits in zip((flat[:half], flat[half:]), orders):
        summed = halving_sum(part, axis, bits).astype(jnp.bfloat16)
        outs.append(halving_gather(summed, axis, bits))
    flat = jnp.concatenate(outs).astype(jnp.float32)
    results, at = [], 0
    for t in terms:
        results.append(flat[at : at + t.size // lane].reshape(t.shape))
        at += t.size // lane
    return results


def body(features, first_filters, second_filters, out_grad):
    blocks, rows, cols = features.shape
    both_pad = extended(jnp.concatenate([features, out_grad]), (("strip", 1),), 1)
    x_pad, dy_pad = both_pad[:blocks], both_pad[blocks:]
    dy_stack = back_stack(dy_pad)
    hidden_grad = chan_sum_scatter(
        conv_back_stacked(dy_stack, second_filters, 1, rows * cols).reshape(-1, rows * cols), "chan"
    ).reshape(-1, rows, cols)
    x_all = chan_gather(x_pad, "chan")
    x_cols = im2col(x_all)
    pre_full = conv_fwd(x_cols, first_filters, rows, cols)
    pre = pre_full.astype(jnp.bfloat16)
    hidden = jax.nn.silu(pre_full).astype(jnp.bfloat16)
    pre_val = pre.astype(jnp.float32)
    sig = jax.nn.sigmoid(pre_val)
    pre_grad = (hidden_grad * sig * (1.0 + pre_val * (1.0 - sig))).astype(jnp.bfloat16)
    both_pad = extended(jnp.concatenate([hidden, pre_grad]), (("strip", 1),), 1)
    h_pad, da_pad = both_pad[:blocks], both_pad[blocks:]
    h_all = chan_gather(h_pad, "chan")
    h_cols = im2col(h_all)
    (second_grad,) = strip_allreduce((filter_grad(out_grad, h_cols),), "strip")
    output = (features.astype(jnp.float32) + conv_fwd(h_cols, second_filters, rows, cols)).astype(jnp.bfloat16)
    (first_grad,) = strip_allreduce((filter_grad(pre_grad, x_cols),), "strip")
    da_stack = back_stack(da_pad)
    input_term = chan_sum_scatter(
        conv_back_stacked(da_stack, first_filters, 1, rows * cols).reshape(-1, rows * cols), "chan"
    ).reshape(-1, rows, cols)
    input_grad = (out_grad.astype(jnp.float32) + input_term).astype(jnp.bfloat16)
    return (output, input_grad, first_grad, second_grad)


def solution(mesh):
    in_specs = (
        P("chan", "strip", None),
        P("chan", None, None, None),
        P("chan", None, None, None),
        P("chan", "strip", None),
    )
    out_specs = (
        P("chan", "strip", None),
        P("chan", "strip", None),
        P("chan", None, None, None),
        P("chan", None, None, None),
    )
    return jax.shard_map(body, mesh=mesh, in_specs=in_specs, out_specs=out_specs, check_vma=False)
```
